128 devices in a mesh: dp: 32 (over y, z, x_hi), mp: 4 (over x_lo, core).
Axes of the slice: x: 4 (x_hi: 2, x_lo: 2; x = x_hi * 2 + x_lo), y: 4, z: 4, core: 2. Of those that a mesh axis runs over, the one named last changes fastest.
Arguments:
- tokens: bfloat16 [8192, 2048], P('dp'), may hold values from -6 to 6
- lengths: int32 [4], replicated, may hold values from 1 to 4096, 8192 in all
- w_query: float32 [2048, 2048], P('dp', 'mp')
- w_key: float32 [2048, 2048], P('dp', 'mp')
- w_value: float32 [2048, 2048], P('dp', 'mp'), may hold values from -0.125 to 0.125
- w_out: float32 [2048, 2048], P('dp', 'mp'), may hold values from -0.125 to 0.125
- w_gate: float32 [2048, 4096], P('dp', 'mp'), may hold values from -0.125 to 0.125
- w_up: float32 [2048, 4096], P('dp', 'mp'), may hold values from -0.125 to 0.125
- w_down: float32 [4096, 2048], P('dp', 'mp'), may hold values from -0.09375 to 0.09375
Outputs:
- layer_out: bfloat16 [8192, 2048], P(('dp', 'mp'))
The draws below stay inside these ranges and needn't reach their ends.
Inputs may be any that keep to these rules, and one draw needn't show every extreme that they name: Every prompt is 1 to 4096 tokens long and one is exactly 4096; the lengths sum to 8192.
All inputs are finite; a program needn't handle non-finite values.
Results may differ from the reference program's by a relative error of at most 0.02.
The reference program's roundings to bfloat16 on the way count: a program that leaves them out, or rounds other values in their place, can miss the bound.
Values may be sent and summed in bfloat16 or wider, within the bound.
No kernel may reach another device: no remote copies, remote signals or barrier semaphores. Data moves between devices by JAX's collectives and lax.ppermute only.
A program may use at most 128 MiB of HBM per device.

```python
import math
import jax
import jax.numpy as jnp
import numpy as np
from jax import lax

D = 2048
FF = 4096
HEAD = 128
PROMPTS = 4
TOK_DEV = 256
HEADS = 16
TOKENS = 8192
REACH = 16
MOST = 4096


def projection_draw(key):
    base_key = jax.random.fold_in(key, 0)
    matrix = jax.random.normal(base_key, (D, D), jnp.float32) * D ** (-0.5)
    return matrix


def draw_w_query(key, part):
    return projection_draw(jax.random.fold_in(key, 11))


def draw_w_key(key, part):
    return projection_draw(jax.random.fold_in(key, 12))


def levels(key, dims, shards, smallest, high):
    factor_of, own = 1.0, jax.random.fold_in(key, 6)
    for axis_at, blocks in shards:
        draws = jnp.exp(jax.random.uniform(jax.random.fold_in(own, axis_at), (blocks,), jnp.float32, smallest / len(shards), high / len(shards)))
        factor_of = factor_of * jnp.repeat(draws, dims[axis_at] // blocks).reshape([-1 if axis == axis_at else 1 for axis in range(len(dims))])
    return factor_of


def split_up(number_of, total, limit, skew):
    portions = [(1 << 20) // math.isqrt(rank ** skew) + 1 for rank in range(2, number_of + 1)]
    surplus, holding = total - limit - (number_of - 1), [1] * (number_of - 1)
    while surplus > 0:
        movable = [i for i in range(number_of - 1) if holding[i] < limit]
        pool, left = sum([portions[i] for i in movable]), surplus
        for i in movable:
            more = min(limit - holding[i], max(1, left * portions[i] // pool), surplus)
            holding[i] = holding[i] + more
            surplus = surplus - more
    return np.array([limit] + holding)


def ragged(own_key, amount, total, limit, slope):
    if amount == 2:
        one = jax.random.randint(own_key, (), max(1, total - limit), min(limit, total - 1) + 1)
        return jnp.stack([one, total - one])
    tallies = jnp.asarray(split_up(amount, total, limit, slope), jnp.int32)
    couples = (amount - 1) // 2
    giver, taker = tallies[1:1 + 2 * couples:2], tallies[2:2 + 2 * couples:2]
    room = jnp.minimum(giver - 1, limit - taker)
    shifted = jax.random.randint(jax.random.fold_in(own_key, 1), (couples,), 0, 1 << 20) % (room + 1)
    tallies = tallies.at[1:1 + 2 * couples:2].set(giver - shifted).at[2:2 + 2 * couples:2].set(taker + shifted)
    return tallies[jax.random.permutation(jax.random.fold_in(own_key, 2), amount)]


def scatter_about(rng, dims, scale, limit, cuts=(), kind=jnp.bfloat16):
    loudness = levels(rng, dims, cuts, -0.22, 0.18) if cuts else 1.0
    array = jax.random.normal(rng, dims, jnp.float32) * scale * loudness
    return jnp.minimum(jnp.maximum(array, -limit), limit).astype(kind)


def setup_inputs(seed: int = 0) -> dict:
    seeds = jax.random.split(jax.random.key(seed), 10)
    tokens = scatter_about(seeds[0], (TOKENS, D), 1.0, 6.0, ((0, 32),))
    lengths = ragged(seeds[1], PROMPTS, TOKENS, MOST, 2).astype(jnp.int32)
    w_query = draw_w_query(jax.random.fold_in(seeds[9], 71), 0)
    w_key = draw_w_key(jax.random.fold_in(seeds[9], 71), 0)
    w_value = scatter_about(seeds[4], (D, D), D ** -0.5, 0.125, ((0, 32), (1, 4)), jnp.float32)
    w_out = scatter_about(seeds[5], (D, D), D ** -0.5, 0.125, ((0, 32), (1, 4)), jnp.float32)
    w_gate = scatter_about(seeds[6], (D, FF), D ** -0.5, 0.125, ((0, 32), (1, 4)), jnp.float32)
    w_up = scatter_about(seeds[7], (D, FF), D ** -0.5, 0.125, ((0, 32), (1, 4)), jnp.float32)
    w_down = scatter_about(seeds[8], (FF, D), FF ** -0.5, 0.09375, ((0, 32), (1, 4)), jnp.float32)
    return dict(tokens=tokens, lengths=lengths, w_query=w_query, w_key=w_key, w_value=w_value, w_out=w_out, w_gate=w_gate, w_up=w_up, w_down=w_down)


epsilon = 1e-05
theta_base = 10000.0

def layer_norm(rows):
    values = rows.astype(jnp.float32)
    centre = lax.optimization_barrier(jnp.mean(values, axis=-1, keepdims=True))
    spread = lax.optimization_barrier(jnp.mean(jnp.square(values - centre), axis=-1, keepdims=True))
    return (values - centre) * lax.rsqrt(spread + epsilon)

def prompt_coords(first, count, lengths):
    where = (first + jnp.arange(count)).astype(jnp.int32)
    ends = jnp.cumsum(lengths).astype(jnp.int32)
    passed = (ends[None, :] <= where[:, None]).astype(jnp.int32)
    prompt = lax.optimization_barrier(jnp.sum(passed, axis=1)).astype(jnp.int32)
    offset = (where - lax.optimization_barrier(jnp.sum(passed * lengths[None, :], axis=1))).astype(jnp.int32)
    prompt = jnp.where(where < 0, -1, prompt).astype(jnp.int32)
    return (prompt, offset, where)

def rotate(values, offset):
    half = values.shape[-1] // 2
    freqs = jnp.power(theta_base, -jnp.arange(half, dtype=jnp.float32) * 2.0 / values.shape[-1])
    angles = offset.astype(jnp.float32)[:, None] * freqs[None, :]
    cosine = jnp.cos(angles)[:, None, :]
    sine = jnp.sin(angles)[:, None, :]
    first_half = values[..., :half]
    second_half = values[..., half:]
    return jnp.concatenate([first_half * cosine - second_half * sine, second_half * cosine + first_half * sine], axis=-1)

def online_step(state, query, keys, values, q_prompt, q_where, k_prompt, k_where):
    accum, total, top = state
    scale = 1.0 / query.shape[-1] ** 0.5
    scores = jnp.einsum('qhd,khd->hqk', query.astype(jnp.float32), keys.astype(jnp.float32)) * scale
    allowed = (q_prompt[:, None] == k_prompt[None, :]) & (k_where[None, :] <= q_where[:, None])
    scores = jnp.where(allowed[None], scores, -jnp.inf)
    new_top = jnp.maximum(top, lax.optimization_barrier(jnp.max(scores, axis=-1, keepdims=True)))
    fade = jnp.exp(top - new_top)
    weights = jnp.exp(scores - new_top)
    probs = weights.astype(jnp.bfloat16)
    product = jnp.einsum('hqk,khd->qhd', probs.astype(jnp.float32), values.astype(jnp.float32))
    accum = accum * jnp.transpose(fade, (1, 0, 2)) + product
    total = total * fade + lax.optimization_barrier(jnp.sum(weights, axis=-1, keepdims=True))
    return (accum, total, new_top)

def reference(tokens, lengths, w_query, w_key, w_value, w_out, w_gate, w_up, w_down):
    half_type = jnp.bfloat16
    normed = layer_norm(tokens).astype(half_type)
    prompt, offset, where = prompt_coords(0, TOKENS, lengths)
    query = jnp.dot(normed, w_query.astype(half_type), preferred_element_type=jnp.float32)
    keys = jnp.dot(normed, w_key.astype(half_type), preferred_element_type=jnp.float32)
    values = jnp.dot(normed, w_value.astype(half_type), preferred_element_type=jnp.float32)
    query = rotate(query.reshape(TOKENS, HEADS, HEAD), offset).astype(half_type)
    keys = rotate(keys.reshape(TOKENS, HEADS, HEAD), offset).astype(half_type)
    values = values.astype(half_type).reshape(TOKENS, HEADS, HEAD)
    margin = REACH * TOK_DEV
    keys_pad = jnp.concatenate([jnp.zeros((margin, HEADS, HEAD), half_type), keys], axis=0)
    values_pad = jnp.concatenate([jnp.zeros((margin, HEADS, HEAD), half_type), values], axis=0)
    k_prompt_pad, k_offset_pad, k_where_pad = prompt_coords(-margin, TOKENS + margin, lengths)

    def one_block(block):
        first = (block * TOK_DEV).astype(jnp.int32)
        q_block = lax.dynamic_slice_in_dim(query, first, TOK_DEV, 0)
        qp = lax.dynamic_slice_in_dim(prompt, first, TOK_DEV, 0)
        qw = lax.dynamic_slice_in_dim(where, first, TOK_DEV, 0)
        state = (jnp.zeros((TOK_DEV, HEADS, HEAD), jnp.float32), jnp.zeros((HEADS, TOK_DEV, 1), jnp.float32), jnp.full((HEADS, TOK_DEV, 1), -jnp.inf, jnp.float32))

        def slot_step(slot, state):
            start = (first + margin - slot * TOK_DEV).astype(jnp.int32)
            k_block = lax.dynamic_slice_in_dim(keys_pad, start, TOK_DEV, 0)
            v_block = lax.dynamic_slice_in_dim(values_pad, start, TOK_DEV, 0)
            kp = lax.dynamic_slice_in_dim(k_prompt_pad, start, TOK_DEV, 0)
            kw = lax.dynamic_slice_in_dim(k_where_pad, start, TOK_DEV, 0)
            return online_step(state, q_block, k_block, v_block, qp, qw, kp, kw)
        accum, total, top = lax.fori_loop(0, REACH + 1, slot_step, state)
        return (accum / jnp.transpose(total, (1, 0, 2))).astype(half_type)
    context = lax.map(one_block, jnp.arange(TOKENS // TOK_DEV, dtype=jnp.int32)).reshape(TOKENS, D)
    attended = jnp.dot(context, w_out.astype(half_type), preferred_element_type=jnp.float32)
    mixed = (tokens.astype(jnp.float32) + attended).astype(half_type)
    normed_two = layer_norm(mixed).astype(half_type)
    gate = jnp.dot(normed_two, w_gate.astype(half_type), preferred_element_type=jnp.float32)
    upper = jnp.dot(normed_two, w_up.astype(half_type), preferred_element_type=jnp.float32)
    hidden = (jax.nn.silu(gate) * upper).astype(half_type)
    mlp_sum = jnp.dot(hidden, w_down.astype(half_type), preferred_element_type=jnp.float32)
    return (mixed.astype(jnp.float32) + mlp_sum).astype(half_type)
```

```python
import jax
import jax.numpy as jnp
from jax import lax
from jax.sharding import PartitionSpec as P

HEAD = 128


epsilon = 1e-05
theta_base = 10000.0


def shifted(value, axis, steps):
    count = lax.axis_size(axis)
    return lax.ppermute(value, axis, [(source, source + steps) for source in range(count - steps)])


def gather_by_exchange(value, axis):
    count = lax.axis_size(axis)
    copies = jnp.broadcast_to(value[None], (count,) + value.shape)
    got = lax.all_to_all(copies, axis, 0, 0, tiled=True)
    return got.reshape((count * value.shape[0],) + value.shape[1:])


def scatter_sum(value, axis):
    count = lax.axis_size(axis)
    pieces = value.reshape((count, value.shape[0] // count) + value.shape[1:])
    got = lax.all_to_all(pieces, axis, 0, 0, tiled=True)
    return jnp.sum(got.astype(jnp.float32), axis=0)


def layer_norm(rows):
    values = rows.astype(jnp.float32)
    centre = jnp.mean(values, axis=-1, keepdims=True)
    spread = jnp.mean(jnp.square(values - centre), axis=-1, keepdims=True)
    return (values - centre) * lax.rsqrt(spread + epsilon)


def prompt_coords(first, count, lengths):
    where = first + jnp.arange(count)
    ends = jnp.cumsum(lengths)
    passed = (ends[None, :] <= where[:, None]).astype(jnp.int32)
    prompt = jnp.sum(passed, axis=1)
    offset = where - jnp.sum(passed * lengths[None, :], axis=1)
    prompt = jnp.where(where < 0, -1, prompt)
    return (prompt, offset, where)


def rotate(values, offset):
    half = values.shape[-1] // 2
    freqs = jnp.power(theta_base, -jnp.arange(half, dtype=jnp.float32) * 2.0 / values.shape[-1])
    angles = offset.astype(jnp.float32)[:, None] * freqs[None, :]
    cosine = jnp.cos(angles)[:, None, :]
    sine = jnp.sin(angles)[:, None, :]
    first_half = values[..., :half]
    second_half = values[..., half:]
    return jnp.concatenate(
        [first_half * cosine - second_half * sine, second_half * cosine + first_half * sine],
        axis=-1,
    )


def on_device(tokens, lengths, w_query, w_key, w_value, w_out, w_gate, w_up, w_down):
    half_type = jnp.bfloat16
    rows = tokens.shape[0]
    narrow = w_query.shape[1]
    units = w_gate.shape[1]
    shard_rows = w_query.shape[0]
    heads_dev = narrow // HEAD
    dp_index = lax.axis_index("dp")
    mp_index = lax.axis_index("mp")
    mp_size = lax.axis_size("mp")
    reach = lax.axis_size("dp") // 2

    qkv_shard = jnp.concatenate(
        [w.astype(half_type) for w in (w_query, w_key, w_value)], axis=1
    )
    rest_shard = jnp.concatenate(
        [
            w_out.astype(half_type),
            w_gate.astype(half_type),
            w_up.astype(half_type),
            w_down.astype(half_type).reshape(shard_rows, -1),
        ],
        axis=1,
    )
    qkv_full = gather_by_exchange(qkv_shard, "dp")
    rest_full = lax.all_gather(rest_shard, "dp", axis=0, tiled=True)

    normed = layer_norm(tokens).astype(half_type)
    joined = jnp.dot(normed, qkv_full, preferred_element_type=jnp.float32)
    q_prompt, q_offset, q_where = prompt_coords(dp_index * rows, rows, lengths)
    shaped = joined.reshape(rows, 3, heads_dev, HEAD)
    query = rotate(shaped[:, 0], q_offset).astype(half_type)
    keys = rotate(shaped[:, 1], q_offset).astype(half_type)
    values = shaped[:, 2].astype(half_type)
    own_first = dp_index * rows
    scale = 1.0 / HEAD**0.5

    def online_step(state, pair, first):
        accum, total, top = state
        k_prompt, k_offset, k_where = prompt_coords(first, rows, lengths)
        scores = (
            jnp.einsum("qhd,khd->hqk", query, pair[0], preferred_element_type=jnp.float32) * scale
        )
        allowed = (q_prompt[:, None] == k_prompt[None, :]) & (k_where[None, :] <= q_where[:, None])
        scores = jnp.where(allowed[None], scores, -jnp.inf)
        new_top = jnp.maximum(top, jnp.max(scores, axis=-1, keepdims=True))
        fade = jnp.exp(top - new_top)
        weights = jnp.exp(scores - new_top)
        probs = weights.astype(half_type)
        product = jnp.einsum("hqk,khd->qhd", probs, pair[1], preferred_element_type=jnp.float32)
        accum = accum * jnp.transpose(fade, (1, 0, 2)) + product
        total = total * fade + jnp.sum(weights, axis=-1, keepdims=True)
        return (accum, total, new_top)

    state = (
        jnp.zeros((rows, heads_dev, HEAD), jnp.float32),
        jnp.zeros((heads_dev, rows, 1), jnp.float32),
        jnp.full((heads_dev, rows, 1), -jnp.inf, jnp.float32),
    )
    held = jnp.stack((keys, values))[None]
    farthest = shifted(held, "dp", reach)
    state = online_step(state, held[0], own_first)
    done = 1
    span = 1
    while span < reach:
        arrived = shifted(held, "dp", span)
        for slot in range(arrived.shape[0]):
            state = online_step(state, arrived[slot], own_first - (done + slot) * rows)
        done += arrived.shape[0]
        held = jnp.concatenate([held, arrived], axis=0)
        span *= 2
    state = online_step(state, farthest[0], own_first - reach * rows)
    accum, total, top = state
    context = (accum / jnp.transpose(total, (1, 0, 2))).astype(half_type).reshape(rows, narrow)

    out_cols = rest_full[:, :narrow]
    server_out = lax.all_to_all(out_cols, "mp", split_axis=0, concat_axis=1, tiled=True)
    partial_out = jnp.dot(context, server_out, preferred_element_type=jnp.float32)
    attended = scatter_sum(partial_out.astype(half_type), "mp")
    slab = rows // mp_size
    own_tokens = lax.dynamic_slice_in_dim(tokens, mp_index * slab, slab, 0)
    mixed = (own_tokens.astype(jnp.float32) + attended).astype(half_type)
    normed_own = layer_norm(mixed).astype(half_type)
    normed_two = gather_by_exchange(normed_own, "mp")

    gate = jnp.dot(normed_two, rest_full[:, narrow : narrow + units], preferred_element_type=jnp.float32)
    upper = jnp.dot(
        normed_two, rest_full[:, narrow + units : narrow + 2 * units], preferred_element_type=jnp.float32
    )
    hidden = (jax.nn.silu(gate) * upper).astype(half_type)
    down_cols = rest_full[:, narrow + 2 * units :].reshape(-1, narrow)
    server_down = lax.all_to_all(down_cols, "mp", split_axis=0, concat_axis=1, tiled=True)
    partial_down = jnp.dot(hidden, server_down, preferred_element_type=jnp.float32)
    share = scatter_sum(partial_down.astype(half_type), "mp")
    return (mixed.astype(jnp.float32) + share).astype(half_type)


def solution(mesh):
    in_specs = (
        P("dp", None),
        P(),
        P("dp", "mp"),
        P("dp", "mp"),
        P("dp", "mp"),
        P("dp", "mp"),
        P("dp", "mp"),
        P("dp", "mp"),
        P("dp", "mp"),
    )
    out_specs = P(("dp", "mp"), None)
    return jax.shard_map(
        on_device, mesh=mesh, in_specs=in_specs, out_specs=out_specs, check_vma=False
    )
```

```python
import jax
import jax.numpy as jnp
from jax import lax
from jax.sharding import Mesh, PartitionSpec as P

HEAD = 128


epsilon = 1e-05
theta_base = 10000.0


def shifted(value, axis, steps):
    count = lax.axis_size(axis)
    return lax.ppermute(value, axis, [(source, source + steps) for source in range(count - steps)])


def gather_by_exchange(value, axis):
    count = lax.axis_size(axis)
    copies = jnp.broadcast_to(value[None], (count,) + value.shape)
    got = lax.all_to_all(copies, axis, 0, 0, tiled=True)
    return got.reshape((count * value.shape[0],) + value.shape[1:])


def scatter_sum(value, axis):
    count = lax.axis_size(axis)
    pieces = value.reshape((count, value.shape[0] // count) + value.shape[1:])
    got = lax.all_to_all(pieces, axis, 0, 0, tiled=True)
    return jnp.sum(got.astype(jnp.float32), axis=0)


def layer_norm(rows):
    values = rows.astype(jnp.float32)
    centre = jnp.mean(values, axis=-1, keepdims=True)
    spread = jnp.mean(jnp.square(values - centre), axis=-1, keepdims=True)
    return (values - centre) * lax.rsqrt(spread + epsilon)


def prompt_coords(first, count, lengths):
    where = first + jnp.arange(count)
    ends = jnp.cumsum(lengths)
    passed = (ends[None, :] <= where[:, None]).astype(jnp.int32)
    prompt = jnp.sum(passed, axis=1)
    offset = where - jnp.sum(passed * lengths[None, :], axis=1)
    prompt = jnp.where(where < 0, -1, prompt)
    return (prompt, offset, where)


def rotate(values, offset):
    half = values.shape[-1] // 2
    freqs = jnp.power(theta_base, -jnp.arange(half, dtype=jnp.float32) * 2.0 / values.shape[-1])
    angles = offset.astype(jnp.float32)[:, None] * freqs[None, :]
    cosine = jnp.cos(angles)[:, None, :]
    sine = jnp.sin(angles)[:, None, :]
    first_half = values[..., :half]
    second_half = values[..., half:]
    return jnp.concatenate(
        [first_half * cosine - second_half * sine, second_half * cosine + first_half * sine],
        axis=-1,
    )


def on_device(tokens, lengths, w_query, w_key, w_value, w_out, w_gate, w_up, w_down):
    half_type = jnp.bfloat16
    dp = ("y", "r")
    mp = "mp"
    rows = tokens.shape[0]
    narrow = w_query.shape[1]
    shard_rows = w_query.shape[0]
    heads_dev = narrow // HEAD
    dp_index = lax.axis_index(dp)
    mp_index = lax.axis_index(mp)
    mp_size = lax.axis_size(mp)
    y_size = lax.axis_size("y")
    r_size = lax.axis_size("r")
    reach = lax.axis_size(dp) // 2

    down_rows = w_down.shape[0]
    per_mp = down_rows // mp_size
    down_shard = lax.all_to_all(
        w_down.astype(half_type).reshape(mp_size, per_mp, narrow), mp, 0, 0, tiled=True
    )
    down_shard = jnp.transpose(down_shard, (1, 0, 2)).reshape(per_mp, mp_size * narrow)
    units_shard = w_gate.shape[1]
    blocks = units_shard // down_rows

    def unit_columns(w):
        pieces = w.astype(half_type).reshape(shard_rows, blocks, mp_size, per_mp)
        pieces = jnp.transpose(pieces, (2, 0, 1, 3))
        got = lax.all_to_all(pieces, mp, 0, 0, tiled=True)
        return jnp.transpose(got, (1, 0, 2, 3)).reshape(shard_rows, mp_size * blocks * per_mp)

    gate_shard = unit_columns(w_gate)
    up_shard = unit_columns(w_up)
    units = gate_shard.shape[1]
    rest_shard = jnp.concatenate(
        [gate_shard, up_shard, down_shard.reshape(shard_rows, -1)], axis=1
    )

    out_full_rows = gather_by_exchange(jnp.transpose(w_out.astype(half_type)), mp)
    out_full_rows = jnp.transpose(out_full_rows)
    swap = [(a * mp_size + b, b * mp_size + a) for a in range(y_size) for b in range(mp_size)]
    out_swapped = lax.ppermute(out_full_rows, ("y", mp), swap)
    server_out = gather_by_exchange(out_swapped, "r")

    kv_shard = jnp.concatenate([w.astype(half_type) for w in (w_key, w_value)], axis=1)
    kv_full = gather_by_exchange(kv_shard, dp)
    q_full = lax.all_gather(w_query.astype(half_type), dp, axis=0, tiled=True)
    rest_full = lax.all_gather(rest_shard, dp, axis=0, tiled=True)

    normed = layer_norm(tokens).astype(half_type)
    joined_kv = jnp.dot(normed, kv_full, preferred_element_type=jnp.float32)
    q_prompt, q_offset, q_where = prompt_coords(dp_index * rows, rows, lengths)
    shaped = joined_kv.reshape(rows, 2, heads_dev, HEAD)
    keys = rotate(shaped[:, 0], q_offset).astype(half_type)
    values = shaped[:, 1].astype(half_type)
    held = jnp.stack((keys, values))[None]
    farthest = shifted(held, dp, reach)
    joined_q = jnp.dot(normed, q_full, preferred_element_type=jnp.float32)
    query = rotate(joined_q.reshape(rows, heads_dev, HEAD), q_offset).astype(half_type)
    own_first = dp_index * rows
    scale = 1.0 / HEAD**0.5

    def online_step(state, pair, first):
        accum, total, top = state
        k_prompt, k_offset, k_where = prompt_coords(first, rows, lengths)
        scores = (
            jnp.einsum("qhd,khd->hqk", query, pair[0], preferred_element_type=jnp.float32) * scale
        )
        allowed = (q_prompt[:, None] == k_prompt[None, :]) & (k_where[None, :] <= q_where[:, None])
        scores = jnp.where(allowed[None], scores, -jnp.inf)
        new_top = jnp.maximum(top, jnp.max(scores, axis=-1, keepdims=True))
        fade = jnp.exp(top - new_top)
        weights = jnp.exp(scores - new_top)
        probs = weights.astype(half_type)
        product = jnp.einsum("hqk,khd->qhd", probs, pair[1], preferred_element_type=jnp.float32)
        accum = accum * jnp.transpose(fade, (1, 0, 2)) + product
        total = total * fade + jnp.sum(weights, axis=-1, keepdims=True)
        return (accum, total, new_top)

    state = (
        jnp.zeros((rows, heads_dev, HEAD), jnp.float32),
        jnp.zeros((heads_dev, rows, 1), jnp.float32),
        jnp.full((heads_dev, rows, 1), -jnp.inf, jnp.float32),
    )
    state = online_step(state, held[0], own_first)
    done = 1
    span = 1
    while span < reach:
        arrived = shifted(held, dp, span)
        if arrived.shape[0] < 4:
            for slot in range(arrived.shape[0]):
                state = online_step(state, arrived[slot], own_first - (done + slot) * rows)
        else:
            def slot_step(slot, state, arrived=arrived, done=done):
                return online_step(state, arrived[slot], own_first - (done + slot) * rows)

            state = lax.fori_loop(0, arrived.shape[0], slot_step, state)
        done += arrived.shape[0]
        held = jnp.concatenate([held, arrived], axis=0)
        span *= 2
    state = online_step(state, farthest[0], own_first - reach * rows)
    accum, total, top = state
    context = (accum / jnp.transpose(total, (1, 0, 2))).astype(half_type).reshape(rows, narrow)

    partial_out = jnp.dot(context, server_out, preferred_element_type=jnp.float32)
    attended = scatter_sum(partial_out.astype(half_type), mp)
    slab = rows // mp_size
    own_tokens = lax.dynamic_slice_in_dim(tokens, mp_index * slab, slab, 0)
    mixed = (own_tokens.astype(jnp.float32) + attended).astype(half_type)
    normed_own = layer_norm(mixed).astype(half_type)
    normed_two = gather_by_exchange(normed_own, mp)

    gate = jnp.dot(normed_two, rest_full[:, :units], preferred_element_type=jnp.float32)
    upper = jnp.dot(normed_two, rest_full[:, units : 2 * units], preferred_element_type=jnp.float32)
    hidden = (jax.nn.silu(gate) * upper).astype(half_type)
    server_down = rest_full[:, 2 * units :].reshape(units, -1)
    partial_down = jnp.dot(hidden, server_down, preferred_element_type=jnp.float32)
    share = scatter_sum(partial_down.astype(half_type), mp)
    return (mixed.astype(jnp.float32) + share).astype(half_type)


def solution(mesh):
    dp_size, mp_size = mesh.devices.shape
    y_size = mesh.devices.shape[0] // 8 if dp_size % 8 == 0 else 1
    fine = Mesh(mesh.devices.reshape(y_size, dp_size // y_size, mp_size), ("y", "r", "mp"))
    dp = ("y", "r")
    in_specs = (
        P(dp, None),
        P(),
        P(dp, "mp"),
        P(dp, "mp"),
        P(dp, "mp"),
        P(dp, "mp"),
        P(dp, "mp"),
        P(dp, "mp"),
        P(dp, "mp"),
    )
    out_specs = P(("y", "r", "mp"), None)
    return jax.shard_map(
        on_device, mesh=fine, in_specs=in_specs, out_specs=out_specs, check_vma=False
    )
```

```python
import jax
import jax.numpy as jnp
from jax import lax
from jax.sharding import Mesh, PartitionSpec as P

HEAD = 128


epsilon = 1e-05
theta_base = 10000.0


def shifted(value, axis, steps):
    count = lax.axis_size(axis)
    return lax.ppermute(value, axis, [(source, source + steps) for source in range(count - steps)])


def gather_by_exchange(value, axis):
    count = lax.axis_size(axis)
    copies = jnp.broadcast_to(value[None], (count,) + value.shape)
    got = lax.all_to_all(copies, axis, 0, 0, tiled=True)
    return got.reshape((count * value.shape[0],) + value.shape[1:])


def scatter_sum(value, axis):
    count = lax.axis_size(axis)
    pieces = value.reshape((count, value.shape[0] // count) + value.shape[1:])
    got = lax.all_to_all(pieces, axis, 0, 0, tiled=True)
    return jnp.sum(got.astype(jnp.float32), axis=0)


def layer_norm(rows):
    values = rows.astype(jnp.float32)
    centre = jnp.mean(values, axis=-1, keepdims=True)
    spread = jnp.mean(jnp.square(values - centre), axis=-1, keepdims=True)
    return (values - centre) * lax.rsqrt(spread + epsilon)


def prompt_coords(first, count, lengths):
    where = first + jnp.arange(count)
    ends = jnp.cumsum(lengths)
    passed = (ends[None, :] <= where[:, None]).astype(jnp.int32)
    prompt = jnp.sum(passed, axis=1)
    offset = where - jnp.sum(passed * lengths[None, :], axis=1)
    prompt = jnp.where(where < 0, -1, prompt)
    return (prompt, offset, where)


def rotate(values, offset):
    half = values.shape[-1] // 2
    freqs = jnp.power(theta_base, -jnp.arange(half, dtype=jnp.float32) * 2.0 / values.shape[-1])
    angles = offset.astype(jnp.float32)[:, None] * freqs[None, :]
    cosine = jnp.cos(angles)[:, None, :]
    sine = jnp.sin(angles)[:, None, :]
    first_half = values[..., :half]
    second_half = values[..., half:]
    return jnp.concatenate(
        [first_half * cosine - second_half * sine, second_half * cosine + first_half * sine],
        axis=-1,
    )


def on_device(tokens, lengths, w_query, w_key, w_value, w_out, w_gate, w_up, w_down):
    half_type = jnp.bfloat16
    dp = ("y", "r")
    mp = "mp"
    rows = tokens.shape[0]
    narrow = w_query.shape[1]
    shard_rows = w_query.shape[0]
    heads_dev = narrow // HEAD
    dp_index = lax.axis_index(dp)
    mp_index = lax.axis_index(mp)
    mp_size = lax.axis_size(mp)
    y_size = lax.axis_size("y")
    r_size = lax.axis_size("r")
    reach = lax.axis_size(dp) // 2

    down_rows = w_down.shape[0]
    per_mp = down_rows // mp_size
    units_shard = w_gate.shape[1]
    blocks = units_shard // down_rows

    def unit_pieces(w):
        pieces = w.astype(half_type).reshape(shard_rows, blocks, mp_size, per_mp)
        return jnp.transpose(pieces, (2, 0, 1, 3))

    outgoing = [
        unit_pieces(w_gate),
        unit_pieces(w_up),
        w_down.astype(half_type).reshape(mp_size, per_mp, narrow),
        jnp.broadcast_to(w_out.astype(half_type)[None], (mp_size,) + w_out.shape),
    ]
    flat = jnp.concatenate([p.reshape(mp_size, -1) for p in outgoing], axis=1)
    got = lax.all_to_all(flat, mp, 0, 0, tiled=True)
    q_shard = w_query.astype(half_type)
    kv_shard = jnp.concatenate([w.astype(half_type) for w in (w_key, w_value)], axis=1)
    got, q_shard, kv_shard = lax.optimization_barrier((got, q_shard, kv_shard))
    pieces = []
    at = 0
    for p in outgoing:
        size = p[0].size
        pieces.append(got[:, at : at + size].reshape(p.shape))
        at += size
    gate_got, up_got, down_got, out_got = pieces

    def unit_columns(got_w):
        return jnp.transpose(got_w, (1, 0, 2, 3)).reshape(shard_rows, mp_size * blocks * per_mp)

    gate_shard = unit_columns(gate_got)
    up_shard = unit_columns(up_got)
    down_shard = jnp.transpose(down_got, (1, 0, 2)).reshape(per_mp, mp_size * narrow)
    units = gate_shard.shape[1]
    rest_shard = jnp.concatenate(
        [gate_shard, up_shard, down_shard.reshape(shard_rows, -1)], axis=1
    )

    out_full_rows = jnp.transpose(out_got, (1, 0, 2)).reshape(shard_rows, mp_size * narrow)
    swap = [(a * mp_size + b, b * mp_size + a) for a in range(y_size) for b in range(mp_size)]
    out_swapped = lax.ppermute(out_full_rows, ("y", mp), swap)
    server_out = gather_by_exchange(out_swapped, "r")

    kv_full = gather_by_exchange(kv_shard, dp)
    q_full = lax.all_gather(q_shard, dp, axis=0, tiled=True)
    rest_full = lax.all_gather(rest_shard, dp, axis=0, tiled=True)

    normed = layer_norm(tokens).astype(half_type)
    joined_kv = jnp.dot(normed, kv_full, preferred_element_type=jnp.float32)
    q_prompt, q_offset, q_where = prompt_coords(dp_index * rows, rows, lengths)
    shaped = joined_kv.reshape(rows, 2, heads_dev, HEAD)
    keys = rotate(shaped[:, 0], q_offset).astype(half_type)
    values = shaped[:, 1].astype(half_type)
    own_pair = jnp.stack((keys, values))
    plane = r_size
    back_one = shifted(own_pair, dp, plane)
    back_two = shifted(own_pair, dp, 2 * plane)
    joined_q = jnp.dot(normed, q_full, preferred_element_type=jnp.float32)
    query = rotate(joined_q.reshape(rows, heads_dev, HEAD), q_offset).astype(half_type)
    own_first = dp_index * rows
    scale = 1.0 / HEAD**0.5

    def online_step(state, pair, first):
        accum, total, top = state
        k_prompt, k_offset, k_where = prompt_coords(first, rows, lengths)
        scores = (
            jnp.einsum("qhd,khd->hqk", query, pair[0], preferred_element_type=jnp.float32) * scale
        )
        allowed = (q_prompt[:, None] == k_prompt[None, :]) & (k_where[None, :] <= q_where[:, None])
        scores = jnp.where(allowed[None], scores, -jnp.inf)
        new_top = jnp.maximum(top, jnp.max(scores, axis=-1, keepdims=True))
        fade = jnp.exp(top - new_top)
        weights = jnp.exp(scores - new_top)
        probs = weights.astype(half_type)
        product = jnp.einsum("hqk,khd->qhd", probs, pair[1], preferred_element_type=jnp.float32)
        accum = accum * jnp.transpose(fade, (1, 0, 2)) + product
        total = total * fade + jnp.sum(weights, axis=-1, keepdims=True)
        return (accum, total, new_top)

    state = (
        jnp.zeros((rows, heads_dev, HEAD), jnp.float32),
        jnp.zeros((heads_dev, rows, 1), jnp.float32),
        jnp.full((heads_dev, rows, 1), -jnp.inf, jnp.float32),
    )
    r_index = lax.axis_index("r")
    later = r_index < jnp.arange(plane)
    nearer = jnp.where(later[:, None, None, None, None], own_pair[None], back_two[None])
    payload = jnp.stack(
        (nearer, jnp.broadcast_to(back_one[None], (plane,) + back_one.shape)), axis=1
    )
    received = lax.all_to_all(payload, "r", 0, 0, tiled=True)
    state = online_step(state, own_pair, own_first)

    def slot_step(back, state):
        source = lax.rem(r_index - back + 2 * plane, plane)
        middle = jnp.logical_and(back > r_index, back <= r_index + plane).astype(jnp.int32)
        pair = received[source, middle]
        return online_step(state, pair, own_first - back * rows)

    state = lax.fori_loop(1, reach + 1, slot_step, state)
    accum, total, top = state
    context = (accum / jnp.transpose(total, (1, 0, 2))).astype(half_type).reshape(rows, narrow)

    partial_out = jnp.dot(context, server_out, preferred_element_type=jnp.float32)
    attended = scatter_sum(partial_out.astype(half_type), mp)
    slab = rows // mp_size
    own_tokens = lax.dynamic_slice_in_dim(tokens, mp_index * slab, slab, 0)
    mixed = (own_tokens.astype(jnp.float32) + attended).astype(half_type)
    normed_own = layer_norm(mixed).astype(half_type)
    normed_two = gather_by_exchange(normed_own, mp)

    gate = jnp.dot(normed_two, rest_full[:, :units], preferred_element_type=jnp.float32)
    upper = jnp.dot(normed_two, rest_full[:, units : 2 * units], preferred_element_type=jnp.float32)
    hidden = (jax.nn.silu(gate) * upper).astype(half_type)
    server_down = rest_full[:, 2 * units :].reshape(units, -1)
    partial_down = jnp.dot(hidden, server_down, preferred_element_type=jnp.float32)
    share = scatter_sum(partial_down.astype(half_type), mp)
    return (mixed.astype(jnp.float32) + share).astype(half_type)


def solution(mesh):
    dp_size, mp_size = mesh.devices.shape
    y_size = mesh.devices.shape[0] // 8 if dp_size % 8 == 0 else 1
    fine = Mesh(mesh.devices.reshape(y_size, dp_size // y_size, mp_size), ("y", "r", "mp"))
    dp = ("y", "r")
    in_specs = (
        P(dp, None),
        P(),
        P(dp, "mp"),
        P(dp, "mp"),
        P(dp, "mp"),
        P(dp, "mp"),
        P(dp, "mp"),
        P(dp, "mp"),
        P(dp, "mp"),
    )
    out_specs = P(("y", "r", "mp"), None)
    return jax.shard_map(
        on_device, mesh=fine, in_specs=in_specs, out_specs=out_specs, check_vma=False
    )
```

```python
import jax
import jax.numpy as jnp
from jax import lax
from jax.sharding import Mesh, PartitionSpec as P

HEAD = 128


epsilon = 1e-05
theta_base = 10000.0


def shifted(value, axis, steps):
    count = lax.axis_size(axis)
    return lax.ppermute(value, axis, [(source, source + steps) for source in range(count - steps)])


def gather_by_exchange(value, axis):
    count = lax.axis_size(axis)
    copies = jnp.broadcast_to(value[None], (count,) + value.shape)
    got = lax.all_to_all(copies, axis, 0, 0, tiled=True)
    return got.reshape((count * value.shape[0],) + value.shape[1:])


def scatter_sum(value, axis):
    count = lax.axis_size(axis)
    pieces = value.reshape((count, value.shape[0] // count) + value.shape[1:])
    got = lax.all_to_all(pieces, axis, 0, 0, tiled=True)
    return jnp.sum(got.astype(jnp.float32), axis=0)


def layer_norm(rows):
    values = rows.astype(jnp.float32)
    centre = jnp.mean(values, axis=-1, keepdims=True)
    spread = jnp.mean(jnp.square(values - centre), axis=-1, keepdims=True)
    return (values - centre) * lax.rsqrt(spread + epsilon)


def prompt_coords(first, count, lengths):
    where = first + jnp.arange(count)
    ends = jnp.cumsum(lengths)
    passed = (ends[None, :] <= where[:, None]).astype(jnp.int32)
    prompt = jnp.sum(passed, axis=1)
    offset = where - jnp.sum(passed * lengths[None, :], axis=1)
    prompt = jnp.where(where < 0, -1, prompt)
    return (prompt, offset, where)


def rotate(values, offset):
    half = values.shape[-1] // 2
    freqs = jnp.power(theta_base, -jnp.arange(half, dtype=jnp.float32) * 2.0 / values.shape[-1])
    angles = offset.astype(jnp.float32)[:, None] * freqs[None, :]
    cosine = jnp.cos(angles)[:, None, :]
    sine = jnp.sin(angles)[:, None, :]
    first_half = values[..., :half]
    second_half = values[..., half:]
    return jnp.concatenate(
        [first_half * cosine - second_half * sine, second_half * cosine + first_half * sine],
        axis=-1,
    )


def on_device(tokens, lengths, w_query, w_key, w_value, w_out, w_gate, w_up, w_down):
    half_type = jnp.bfloat16
    dp = ("y", "r")
    mp = "mp"
    rows = tokens.shape[0]
    narrow = w_query.shape[1]
    shard_rows = w_query.shape[0]
    heads_dev = narrow // HEAD
    dp_index = lax.axis_index(dp)
    mp_index = lax.axis_index(mp)
    mp_size = lax.axis_size(mp)
    y_size = lax.axis_size("y")
    r_size = lax.axis_size("r")
    reach = lax.axis_size(dp) // 2

    down_rows = w_down.shape[0]
    per_mp = down_rows // mp_size
    units_shard = w_gate.shape[1]
    blocks = units_shard // down_rows

    def unit_pieces(w):
        pieces = w.astype(half_type).reshape(shard_rows, blocks, mp_size, per_mp)
        return jnp.transpose(pieces, (2, 0, 1, 3))

    outgoing = [
        unit_pieces(w_gate),
        unit_pieces(w_up),
        w_down.astype(half_type).reshape(mp_size, per_mp, narrow),
        jnp.broadcast_to(w_out.astype(half_type)[None], (mp_size,) + w_out.shape),
    ]
    flat = jnp.concatenate([p.reshape(mp_size, -1) for p in outgoing], axis=1)
    got = lax.all_to_all(flat, mp, 0, 0, tiled=True)
    qkv_shard = jnp.concatenate([w.astype(half_type) for w in (w_key, w_value, w_query)], axis=1)
    got, qkv_shard = lax.optimization_barrier((got, qkv_shard))
    pieces = []
    at = 0
    for p in outgoing:
        size = p[0].size
        pieces.append(got[:, at : at + size].reshape(p.shape))
        at += size
    gate_got, up_got, down_got, out_got = pieces

    def unit_columns(got_w):
        return jnp.transpose(got_w, (1, 0, 2, 3)).reshape(shard_rows, mp_size * blocks * per_mp)

    gate_shard = unit_columns(gate_got)
    up_shard = unit_columns(up_got)
    down_shard = jnp.transpose(down_got, (1, 0, 2)).reshape(per_mp, mp_size * narrow)
    units = gate_shard.shape[1]
    rest_shard = jnp.concatenate(
        [gate_shard, up_shard, down_shard.reshape(shard_rows, -1)], axis=1
    )

    out_full_rows = jnp.transpose(out_got, (1, 0, 2)).reshape(shard_rows, mp_size * narrow)
    swap = [(a * mp_size + b, b * mp_size + a) for a in range(y_size) for b in range(mp_size)]
    out_swapped = lax.ppermute(out_full_rows, ("y", mp), swap)
    server_out = gather_by_exchange(out_swapped, "r")

    qkv_full = gather_by_exchange(qkv_shard, dp)
    kv_full = qkv_full[:, : 2 * narrow]
    q_full = qkv_full[:, 2 * narrow :]
    rest_full = lax.all_gather(rest_shard, dp, axis=0, tiled=True)

    normed = layer_norm(tokens).astype(half_type)
    joined_kv = jnp.dot(normed, kv_full, preferred_element_type=jnp.float32)
    q_prompt, q_offset, q_where = prompt_coords(dp_index * rows, rows, lengths)
    shaped = joined_kv.reshape(rows, 2, heads_dev, HEAD)
    keys = rotate(shaped[:, 0], q_offset).astype(half_type)
    values = shaped[:, 1].astype(half_type)
    own_pair = jnp.stack((keys, values))
    plane = r_size
    back_one = shifted(own_pair, dp, plane)
    back_two = shifted(own_pair, dp, 2 * plane)
    joined_q = jnp.dot(normed, q_full, preferred_element_type=jnp.float32)
    query = rotate(joined_q.reshape(rows, heads_dev, HEAD), q_offset).astype(half_type)
    own_first = dp_index * rows
    scale = 1.0 / HEAD**0.5

    def online_step(state, pair, first):
        accum, total, top = state
        k_prompt, k_offset, k_where = prompt_coords(first, rows, lengths)
        scores = (
            jnp.einsum("qhd,khd->hqk", query, pair[0], preferred_element_type=jnp.float32) * scale
        )
        allowed = (q_prompt[:, None] == k_prompt[None, :]) & (k_where[None, :] <= q_where[:, None])
        scores = jnp.where(allowed[None], scores, -jnp.inf)
        new_top = jnp.maximum(top, jnp.max(scores, axis=-1, keepdims=True))
        fade = jnp.exp(top - new_top)
        weights = jnp.exp(scores - new_top)
        probs = weights.astype(half_type)
        product = jnp.einsum("hqk,khd->qhd", probs, pair[1], preferred_element_type=jnp.float32)
        accum = accum * jnp.transpose(fade, (1, 0, 2)) + product
        total = total * fade + jnp.sum(weights, axis=-1, keepdims=True)
        return (accum, total, new_top)

    state = (
        jnp.zeros((rows, heads_dev, HEAD), jnp.float32),
        jnp.zeros((heads_dev, rows, 1), jnp.float32),
        jnp.full((heads_dev, rows, 1), -jnp.inf, jnp.float32),
    )
    r_index = lax.axis_index("r")
    later = r_index < jnp.arange(plane)
    nearer = jnp.where(later[:, None, None, None, None], own_pair[None], back_two[None])
    payload = jnp.stack(
        (nearer, jnp.broadcast_to(back_one[None], (plane,) + back_one.shape)), axis=1
    )
    received = lax.all_to_all(payload, "r", 0, 0, tiled=True)
    received, rest_full = lax.optimization_barrier((received, rest_full))
    state = online_step(state, own_pair, own_first)

    def slot_step(back, state):
        source = lax.rem(r_index - back + 2 * plane, plane)
        middle = jnp.logical_and(back > r_index, back <= r_index + plane).astype(jnp.int32)
        pair = received[source, middle]
        return online_step(state, pair, own_first - back * rows)

    state = lax.fori_loop(1, reach + 1, slot_step, state)
    accum, total, top = state
    context = (accum / jnp.transpose(total, (1, 0, 2))).astype(half_type).reshape(rows, narrow)

    partial_out = jnp.dot(context, server_out, preferred_element_type=jnp.float32)
    attended = scatter_sum(partial_out.astype(half_type), mp)
    slab = rows // mp_size
    own_tokens = lax.dynamic_slice_in_dim(tokens, mp_index * slab, slab, 0)
    mixed = (own_tokens.astype(jnp.float32) + attended).astype(half_type)
    normed_own = layer_norm(mixed).astype(half_type)
    normed_two = gather_by_exchange(normed_own, mp)

    gate = jnp.dot(normed_two, rest_full[:, :units], preferred_element_type=jnp.float32)
    upper = jnp.dot(normed_two, rest_full[:, units : 2 * units], preferred_element_type=jnp.float32)
    hidden = (jax.nn.silu(gate) * upper).astype(half_type)
    server_down = rest_full[:, 2 * units :].reshape(units, -1)
    partial_down = jnp.dot(hidden, server_down, preferred_element_type=jnp.float32)
    share = scatter_sum(partial_down.astype(half_type), mp)
    return (mixed.astype(jnp.float32) + share).astype(half_type)


def solution(mesh):
    dp_size, mp_size = mesh.devices.shape
    y_size = mesh.devices.shape[0] // 8 if dp_size % 8 == 0 else 1
    fine = Mesh(mesh.devices.reshape(y_size, dp_size // y_size, mp_size), ("y", "r", "mp"))
    dp = ("y", "r")
    in_specs = (
        P(dp, None),
        P(),
        P(dp, "mp"),
        P(dp, "mp"),
        P(dp, "mp"),
        P(dp, "mp"),
        P(dp, "mp"),
        P(dp, "mp"),
        P(dp, "mp"),
    )
    out_specs = P(("y", "r", "mp"), None)
    return jax.shard_map(
        on_device, mesh=fine, in_specs=in_specs, out_specs=out_specs, check_vma=False
    )
```

```python
import jax
import jax.numpy as jnp
from jax import lax
from jax.sharding import Mesh, PartitionSpec as P

HEAD = 128


epsilon = 1e-05
theta_base = 10000.0


def shifted(value, axis, steps):
    count = lax.axis_size(axis)
    return lax.ppermute(value, axis, [(source, source + steps) for source in range(count - steps)])


def gather_by_exchange(value, axis):
    count = lax.axis_size(axis)
    copies = jnp.broadcast_to(value[None], (count,) + value.shape)
    got = lax.all_to_all(copies, axis, 0, 0, tiled=True)
    return got.reshape((count * value.shape[0],) + value.shape[1:])


def scatter_sum(value, axis):
    count = lax.axis_size(axis)
    pieces = value.reshape((count, value.shape[0] // count) + value.shape[1:])
    got = lax.all_to_all(pieces, axis, 0, 0, tiled=True)
    return jnp.sum(got.astype(jnp.float32), axis=0)


def layer_norm(rows):
    values = rows.astype(jnp.float32)
    centre = jnp.mean(values, axis=-1, keepdims=True)
    spread = jnp.mean(jnp.square(values - centre), axis=-1, keepdims=True)
    return (values - centre) * lax.rsqrt(spread + epsilon)


def prompt_coords(first, count, lengths):
    where = first + jnp.arange(count)
    ends = jnp.cumsum(lengths)
    passed = (ends[None, :] <= where[:, None]).astype(jnp.int32)
    prompt = jnp.sum(passed, axis=1)
    offset = where - jnp.sum(passed * lengths[None, :], axis=1)
    prompt = jnp.where(where < 0, -1, prompt)
    return (prompt, offset, where)


def rotate(values, offset):
    half = values.shape[-1] // 2
    freqs = jnp.power(theta_base, -jnp.arange(half, dtype=jnp.float32) * 2.0 / values.shape[-1])
    angles = offset.astype(jnp.float32)[:, None] * freqs[None, :]
    cosine = jnp.cos(angles)[:, None, :]
    sine = jnp.sin(angles)[:, None, :]
    first_half = values[..., :half]
    second_half = values[..., half:]
    return jnp.concatenate(
        [first_half * cosine - second_half * sine, second_half * cosine + first_half * sine],
        axis=-1,
    )


def on_device(tokens, lengths, w_query, w_key, w_value, w_out, w_gate, w_up, w_down):
    half_type = jnp.bfloat16
    dp = ("y", "r")
    mp = "mp"
    rows = tokens.shape[0]
    narrow = w_query.shape[1]
    shard_rows = w_query.shape[0]
    heads_dev = narrow // HEAD
    dp_index = lax.axis_index(dp)
    mp_index = lax.axis_index(mp)
    mp_size = lax.axis_size(mp)
    y_size = lax.axis_size("y")
    r_size = lax.axis_size("r")
    reach = lax.axis_size(dp) // 2

    down_rows = w_down.shape[0]
    per_mp = down_rows // mp_size
    units_shard = w_gate.shape[1]
    blocks = units_shard // down_rows

    def unit_pieces(w):
        pieces = w.astype(half_type).reshape(shard_rows, blocks, mp_size, per_mp)
        return jnp.transpose(pieces, (2, 0, 1, 3))

    outgoing = [
        unit_pieces(w_gate),
        unit_pieces(w_up),
        w_down.astype(half_type).reshape(mp_size, per_mp, narrow),
        jnp.broadcast_to(w_out.astype(half_type)[None], (mp_size,) + w_out.shape),
    ]
    flat = jnp.concatenate([p.reshape(mp_size, -1) for p in outgoing], axis=1)
    got = lax.all_to_all(flat, mp, 0, 0, tiled=True)
    qkv_shard = jnp.concatenate([w.astype(half_type) for w in (w_key, w_value, w_query)], axis=1)
    got, qkv_shard = lax.optimization_barrier((got, qkv_shard))
    pieces = []
    at = 0
    for p in outgoing:
        size = p[0].size
        pieces.append(got[:, at : at + size].reshape(p.shape))
        at += size
    gate_got, up_got, down_got, out_got = pieces

    def unit_columns(got_w):
        return jnp.transpose(got_w, (1, 0, 2, 3)).reshape(shard_rows, mp_size * blocks * per_mp)

    gate_shard = unit_columns(gate_got)
    up_shard = unit_columns(up_got)
    down_shard = jnp.transpose(down_got, (1, 0, 2)).reshape(per_mp, mp_size * narrow)
    units = gate_shard.shape[1]
    rest_shard = jnp.concatenate(
        [gate_shard, up_shard, down_shard.reshape(shard_rows, -1)], axis=1
    )

    out_full_rows = jnp.transpose(out_got, (1, 0, 2)).reshape(shard_rows, mp_size * narrow)
    swap = [(a * mp_size + b, b * mp_size + a) for a in range(y_size) for b in range(mp_size)]
    out_swapped = lax.ppermute(out_full_rows, ("y", mp), swap)
    server_out = gather_by_exchange(out_swapped, "r")

    qkv_full = gather_by_exchange(qkv_shard, dp)
    kv_full = qkv_full[:, : 2 * narrow]
    q_full = qkv_full[:, 2 * narrow :]
    rest_full = lax.all_gather(rest_shard, dp, axis=0, tiled=True)

    normed = layer_norm(tokens).astype(half_type)
    joined_kv = jnp.dot(normed, kv_full, preferred_element_type=jnp.float32)
    q_prompt, q_offset, q_where = prompt_coords(dp_index * rows, rows, lengths)
    shaped = joined_kv.reshape(rows, 2, heads_dev, HEAD)
    keys = rotate(shaped[:, 0], q_offset).astype(half_type)
    values = shaped[:, 1].astype(half_type)
    own_pair = jnp.transpose(jnp.stack((keys, values)), (0, 2, 1, 3))
    plane = r_size
    back_one = shifted(own_pair, dp, plane)
    back_two = shifted(own_pair, dp, 2 * plane)
    joined_q = jnp.dot(normed, q_full, preferred_element_type=jnp.float32)
    query = rotate(joined_q.reshape(rows, heads_dev, HEAD), q_offset).astype(half_type)
    query = jnp.transpose(query, (1, 0, 2))
    own_first = dp_index * rows
    scale = 1.0 / HEAD**0.5

    def online_step(state, pair, first):
        accum, total, top = state
        k_prompt, k_offset, k_where = prompt_coords(first, rows, lengths)
        scores = (
            jnp.einsum("hqd,hkd->hqk", query, pair[0], preferred_element_type=jnp.float32) * scale
        )
        allowed = (q_prompt[:, None] == k_prompt[None, :]) & (k_where[None, :] <= q_where[:, None])
        scores = jnp.where(allowed[None], scores, -jnp.inf)
        new_top = jnp.maximum(top, jnp.max(scores, axis=-1, keepdims=True))
        fade = jnp.exp(top - new_top)
        weights = jnp.exp(scores - new_top)
        probs = weights.astype(half_type)
        product = jnp.einsum("hqk,hkd->hqd", probs, pair[1], preferred_element_type=jnp.float32)
        accum = accum * fade + product
        total = total * fade + jnp.sum(weights, axis=-1, keepdims=True)
        return (accum, total, new_top)

    state = (
        jnp.zeros((heads_dev, rows, HEAD), jnp.float32),
        jnp.zeros((heads_dev, rows, 1), jnp.float32),
        jnp.full((heads_dev, rows, 1), -jnp.inf, jnp.float32),
    )
    r_index = lax.axis_index("r")
    later = r_index < jnp.arange(plane)
    nearer = jnp.where(later[:, None, None, None, None], own_pair[None], back_two[None])
    payload = jnp.stack(
        (nearer, jnp.broadcast_to(back_one[None], (plane,) + back_one.shape)), axis=1
    )
    received = lax.all_to_all(payload, "r", 0, 0, tiled=True)
    server_gate = rest_full[:, :units]
    server_up = rest_full[:, units : 2 * units]
    server_down = rest_full[:, 2 * units :].reshape(units, -1)
    received, server_gate, server_up, server_down = lax.optimization_barrier(
        (received, server_gate, server_up, server_down)
    )
    state = online_step(state, own_pair, own_first)

    def slot_step(back, state):
        source = lax.rem(r_index - back + 2 * plane, plane)
        middle = jnp.logical_and(back > r_index, back <= r_index + plane).astype(jnp.int32)
        pair = received[source, middle]
        return online_step(state, pair, own_first - back * rows)

    state = lax.fori_loop(1, reach + 1, slot_step, state)
    accum, total, top = state
    context = jnp.transpose((accum / total).astype(half_type), (1, 0, 2)).reshape(rows, narrow)

    partial_out = jnp.dot(context, server_out, preferred_element_type=jnp.float32)
    attended = scatter_sum(partial_out.astype(half_type), mp)
    slab = rows // mp_size
    own_tokens = lax.dynamic_slice_in_dim(tokens, mp_index * slab, slab, 0)
    mixed = (own_tokens.astype(jnp.float32) + attended).astype(half_type)
    normed_own = layer_norm(mixed).astype(half_type)
    normed_two = gather_by_exchange(normed_own, mp)

    gate = jnp.dot(normed_two, server_gate, preferred_element_type=jnp.float32)
    upper = jnp.dot(normed_two, server_up, preferred_element_type=jnp.float32)
    hidden = (jax.nn.silu(gate) * upper).astype(half_type)
    partial_down = jnp.dot(hidden, server_down, preferred_element_type=jnp.float32)
    share = scatter_sum(partial_down.astype(half_type), mp)
    return (mixed.astype(jnp.float32) + share).astype(half_type)


def solution(mesh):
    dp_size, mp_size = mesh.devices.shape
    y_size = mesh.devices.shape[0] // 8 if dp_size % 8 == 0 else 1
    fine = Mesh(mesh.devices.reshape(y_size, dp_size // y_size, mp_size), ("y", "r", "mp"))
    dp = ("y", "r")
    in_specs = (
        P(dp, None),
        P(),
        P(dp, "mp"),
        P(dp, "mp"),
        P(dp, "mp"),
        P(dp, "mp"),
        P(dp, "mp"),
        P(dp, "mp"),
        P(dp, "mp"),
    )
    out_specs = P(("y", "r", "mp"), None)
    return jax.shard_map(
        on_device, mesh=fine, in_specs=in_specs, out_specs=out_specs, check_vma=False
    )
```

```python
import jax
import jax.numpy as jnp
from jax import lax
from jax.sharding import Mesh, PartitionSpec as P

HEAD = 128


epsilon = 1e-05
theta_base = 10000.0


def shifted(value, axis, steps):
    count = lax.axis_size(axis)
    return lax.ppermute(value, axis, [(source, source + steps) for source in range(count - steps)])


def gather_by_exchange(value, axis):
    count = lax.axis_size(axis)
    copies = jnp.broadcast_to(value[None], (count,) + value.shape)
    got = lax.all_to_all(copies, axis, 0, 0, tiled=True)
    return got.reshape((count * value.shape[0],) + value.shape[1:])


def scatter_sum(value, axis):
    count = lax.axis_size(axis)
    pieces = value.reshape((count, value.shape[0] // count) + value.shape[1:])
    got = lax.all_to_all(pieces, axis, 0, 0, tiled=True)
    return jnp.sum(got.astype(jnp.float32), axis=0)


def layer_norm(rows):
    values = rows.astype(jnp.float32)
    centre = jnp.mean(values, axis=-1, keepdims=True)
    spread = jnp.mean(jnp.square(values - centre), axis=-1, keepdims=True)
    return (values - centre) * lax.rsqrt(spread + epsilon)


def prompt_coords(first, count, lengths):
    where = first + jnp.arange(count)
    ends = jnp.cumsum(lengths)
    passed = (ends[None, :] <= where[:, None]).astype(jnp.int32)
    prompt = jnp.sum(passed, axis=1)
    offset = where - jnp.sum(passed * lengths[None, :], axis=1)
    prompt = jnp.where(where < 0, -1, prompt)
    return (prompt, offset, where)


def rotate(values, offset):
    half = values.shape[-1] // 2
    freqs = jnp.power(theta_base, -jnp.arange(half, dtype=jnp.float32) * 2.0 / values.shape[-1])
    angles = offset.astype(jnp.float32)[:, None] * freqs[None, :]
    cosine = jnp.cos(angles)[:, None, :]
    sine = jnp.sin(angles)[:, None, :]
    first_half = values[..., :half]
    second_half = values[..., half:]
    return jnp.concatenate(
        [first_half * cosine - second_half * sine, second_half * cosine + first_half * sine],
        axis=-1,
    )


def on_device(tokens, lengths, w_query, w_key, w_value, w_out, w_gate, w_up, w_down):
    half_type = jnp.bfloat16
    dp = ("y", "r")
    mp = "mp"
    rows = tokens.shape[0]
    narrow = w_query.shape[1]
    shard_rows = w_query.shape[0]
    heads_dev = narrow // HEAD
    dp_index = lax.axis_index(dp)
    mp_index = lax.axis_index(mp)
    mp_size = lax.axis_size(mp)
    y_size = lax.axis_size("y")
    r_size = lax.axis_size("r")
    reach = lax.axis_size(dp) // 2

    down_rows = w_down.shape[0]
    per_mp = down_rows // mp_size
    units_shard = w_gate.shape[1]
    blocks = units_shard // down_rows

    def unit_pieces(w):
        pieces = w.astype(half_type).reshape(shard_rows, blocks, mp_size, per_mp)
        return jnp.transpose(pieces, (2, 0, 1, 3))

    outgoing = [
        unit_pieces(w_gate),
        unit_pieces(w_up),
        w_down.astype(half_type).reshape(mp_size, per_mp, narrow),
        jnp.broadcast_to(w_out.astype(half_type)[None], (mp_size,) + w_out.shape),
    ]
    flat = jnp.concatenate([p.reshape(mp_size, -1) for p in outgoing], axis=1)
    got = lax.all_to_all(flat, mp, 0, 0, tiled=True)
    kv_shard = jnp.concatenate([w.astype(half_type) for w in (w_key, w_value)], axis=1)
    got, kv_shard = lax.optimization_barrier((got, kv_shard))
    pieces = []
    at = 0
    for p in outgoing:
        size = p[0].size
        pieces.append(got[:, at : at + size].reshape(p.shape))
        at += size
    gate_got, up_got, down_got, out_got = pieces

    def unit_columns(got_w):
        return jnp.transpose(got_w, (1, 0, 2, 3)).reshape(shard_rows, mp_size * blocks * per_mp)

    gate_shard = unit_columns(gate_got)
    up_shard = unit_columns(up_got)
    down_shard = jnp.transpose(down_got, (1, 0, 2)).reshape(per_mp, mp_size * narrow)
    units = gate_shard.shape[1]
    rest_shard = jnp.concatenate(
        [w_query.astype(half_type), gate_shard, up_shard, down_shard.reshape(shard_rows, -1)], axis=1
    )

    out_full_rows = jnp.transpose(out_got, (1, 0, 2)).reshape(shard_rows, mp_size * narrow)
    swap = [(a * mp_size + b, b * mp_size + a) for a in range(y_size) for b in range(mp_size)]
    out_swapped = lax.ppermute(out_full_rows, ("y", mp), swap)
    server_out = gather_by_exchange(out_swapped, "r")

    kv_full = gather_by_exchange(kv_shard, dp)
    rest_full = lax.all_gather(rest_shard, dp, axis=0, tiled=True)

    normed = layer_norm(tokens).astype(half_type)
    joined_kv = jnp.dot(normed, kv_full, preferred_element_type=jnp.float32)
    q_prompt, q_offset, q_where = prompt_coords(dp_index * rows, rows, lengths)
    shaped = joined_kv.reshape(rows, 2, heads_dev, HEAD)
    keys = rotate(shaped[:, 0], q_offset).astype(half_type)
    values = shaped[:, 1].astype(half_type)
    own_pair = jnp.transpose(jnp.stack((keys, values)), (0, 2, 1, 3))
    plane = r_size
    back_one = shifted(own_pair, dp, plane)
    back_two = shifted(own_pair, dp, 2 * plane)
    own_first = dp_index * rows
    scale = 1.0 / HEAD**0.5

    def online_step(state, pair, first):
        accum, total, top = state
        k_prompt, k_offset, k_where = prompt_coords(first, rows, lengths)
        scores = (
            jnp.einsum("hqd,hkd->hqk", query, pair[0], preferred_element_type=jnp.float32) * scale
        )
        allowed = (q_prompt[:, None] == k_prompt[None, :]) & (k_where[None, :] <= q_where[:, None])
        scores = jnp.where(allowed[None], scores, -jnp.inf)
        new_top = jnp.maximum(top, jnp.max(scores, axis=-1, keepdims=True))
        fade = jnp.exp(top - new_top)
        weights = jnp.exp(scores - new_top)
        probs = weights.astype(half_type)
        product = jnp.einsum("hqk,hkd->hqd", probs, pair[1], preferred_element_type=jnp.float32)
        accum = accum * fade + product
        total = total * fade + jnp.sum(weights, axis=-1, keepdims=True)
        return (accum, total, new_top)

    state = (
        jnp.zeros((heads_dev, rows, HEAD), jnp.float32),
        jnp.zeros((heads_dev, rows, 1), jnp.float32),
        jnp.full((heads_dev, rows, 1), -jnp.inf, jnp.float32),
    )
    r_index = lax.axis_index("r")
    later = r_index < jnp.arange(plane)
    nearer = jnp.where(later[:, None, None, None, None], own_pair[None], back_two[None])
    payload = jnp.stack(
        (nearer, jnp.broadcast_to(back_one[None], (plane,) + back_one.shape)), axis=1
    )
    received = lax.all_to_all(payload, "r", 0, 0, tiled=True)
    q_full = rest_full[:, :narrow]
    server_gate = rest_full[:, narrow : narrow + units]
    server_up = rest_full[:, narrow + units : narrow + 2 * units]
    server_down = rest_full[:, narrow + 2 * units :].reshape(units, -1)
    received, q_full, server_gate, server_up, server_down = lax.optimization_barrier(
        (received, q_full, server_gate, server_up, server_down)
    )
    joined_q = jnp.dot(normed, q_full, preferred_element_type=jnp.float32)
    query = rotate(joined_q.reshape(rows, heads_dev, HEAD), q_offset).astype(half_type)
    query = jnp.transpose(query, (1, 0, 2))
    state = online_step(state, own_pair, own_first)

    def slot_step(back, state):
        source = lax.rem(r_index - back + 2 * plane, plane)
        middle = jnp.logical_and(back > r_index, back <= r_index + plane).astype(jnp.int32)
        pair = received[source, middle]
        return online_step(state, pair, own_first - back * rows)

    state = lax.fori_loop(1, reach + 1, slot_step, state)
    accum, total, top = state
    context = jnp.transpose((accum / total).astype(half_type), (1, 0, 2)).reshape(rows, narrow)

    partial_out = jnp.dot(context, server_out, preferred_element_type=jnp.float32)
    attended = scatter_sum(partial_out.astype(half_type), mp)
    slab = rows // mp_size
    own_tokens = lax.dynamic_slice_in_dim(tokens, mp_index * slab, slab, 0)
    mixed = (own_tokens.astype(jnp.float32) + attended).astype(half_type)
    normed_own = layer_norm(mixed).astype(half_type)
    normed_two = gather_by_exchange(normed_own, mp)

    gate = jnp.dot(normed_two, server_gate, preferred_element_type=jnp.float32)
    upper = jnp.dot(normed_two, server_up, preferred_element_type=jnp.float32)
    hidden = (jax.nn.silu(gate) * upper).astype(half_type)
    partial_down = jnp.dot(hidden, server_down, preferred_element_type=jnp.float32)
    share = scatter_sum(partial_down.astype(half_type), mp)
    return (mixed.astype(jnp.float32) + share).astype(half_type)


def solution(mesh):
    dp_size, mp_size = mesh.devices.shape
    y_size = mesh.devices.shape[0] // 8 if dp_size % 8 == 0 else 1
    fine = Mesh(mesh.devices.reshape(y_size, dp_size // y_size, mp_size), ("y", "r", "mp"))
    dp = ("y", "r")
    in_specs = (
        P(dp, None),
        P(),
        P(dp, "mp"),
        P(dp, "mp"),
        P(dp, "mp"),
        P(dp, "mp"),
        P(dp, "mp"),
        P(dp, "mp"),
        P(dp, "mp"),
    )
    out_specs = P(("y", "r", "mp"), None)
    return jax.shard_map(
        on_device, mesh=fine, in_specs=in_specs, out_specs=out_specs, check_vma=False
    )
```

```python
import jax
import jax.numpy as jnp
from jax import lax
from jax.sharding import Mesh, PartitionSpec as P
from jax.experimental import pallas as pl
from jax.experimental.pallas import tpu as pltpu

HEAD = 128


epsilon = 1e-05
theta_base = 10000.0


def shifted(value, axis, steps):
    count = lax.axis_size(axis)
    return lax.ppermute(value, axis, [(source, source + steps) for source in range(count - steps)])


def gather_by_exchange(value, axis):
    count = lax.axis_size(axis)
    copies = jnp.broadcast_to(value[None], (count,) + value.shape)
    got = lax.all_to_all(copies, axis, 0, 0, tiled=True)
    return got.reshape((count * value.shape[0],) + value.shape[1:])


def scatter_sum(value, axis):
    count = lax.axis_size(axis)
    pieces = value.reshape((count, value.shape[0] // count) + value.shape[1:])
    got = lax.all_to_all(pieces, axis, 0, 0, tiled=True)
    return jnp.sum(got.astype(jnp.float32), axis=0)


def layer_norm(rows):
    values = rows.astype(jnp.float32)
    centre = jnp.mean(values, axis=-1, keepdims=True)
    spread = jnp.mean(jnp.square(values - centre), axis=-1, keepdims=True)
    return (values - centre) * lax.rsqrt(spread + epsilon)


def prompt_coords(first, count, lengths):
    where = first + jnp.arange(count)
    ends = jnp.cumsum(lengths)
    passed = (ends[None, :] <= where[:, None]).astype(jnp.int32)
    prompt = jnp.sum(passed, axis=1)
    offset = where - jnp.sum(passed * lengths[None, :], axis=1)
    prompt = jnp.where(where < 0, -1, prompt)
    return (prompt, offset, where)


def rotate(values, offset):
    half = values.shape[-1] // 2
    freqs = jnp.power(theta_base, -jnp.arange(half, dtype=jnp.float32) * 2.0 / values.shape[-1])
    angles = offset.astype(jnp.float32)[:, None] * freqs[None, :]
    cosine = jnp.cos(angles)[:, None, :]
    sine = jnp.sin(angles)[:, None, :]
    first_half = values[..., :half]
    second_half = values[..., half:]
    return jnp.concatenate(
        [first_half * cosine - second_half * sine, second_half * cosine + first_half * sine],
        axis=-1,
    )


def attend_kernel(meta, query_ref, own_ref, received_ref, qp_ref, qw_ref, kp_ref, kw_ref, out_ref):
    r_index = meta[0]
    plane = received_ref.shape[0]
    steps = kp_ref.shape[0]
    heads = query_ref.shape[0]
    scale = 1.0 / query_ref.shape[-1] ** 0.5
    qp = qp_ref[...]
    qw = qw_ref[...]

    def one_step(head, keys, values, back, carry):
        accum, total, top = carry
        scores = lax.dot_general(
            query_ref[head], keys, (((1,), (1,)), ((), ())), preferred_element_type=jnp.float32
        ) * scale
        allowed = (qp == kp_ref[back]) & (kw_ref[back] <= qw)
        scores = jnp.where(allowed, scores, -jnp.inf)
        new_top = jnp.maximum(top, jnp.max(scores, axis=1, keepdims=True))
        fade = jnp.exp(top - new_top)
        weights = jnp.exp(scores - new_top)
        probs = weights.astype(jnp.bfloat16)
        product = jnp.dot(probs, values, preferred_element_type=jnp.float32)
        accum = accum * fade + product
        total = total * fade + jnp.sum(weights, axis=1, keepdims=True)
        return (accum, total, new_top)

    for head in range(heads):
        rows, width = query_ref.shape[1], query_ref.shape[2]
        carry = (
            jnp.zeros((rows, width), jnp.float32),
            jnp.zeros((rows, 1), jnp.float32),
            jnp.full((rows, 1), -jnp.inf, jnp.float32),
        )
        carry = one_step(head, own_ref[0, head], own_ref[1, head], 0, carry)

        def body(back, carry, head=head):
            source = lax.rem(r_index - back + 2 * plane, plane)
            middle = jnp.logical_and(back > r_index, back <= r_index + plane).astype(jnp.int32)
            keys = received_ref[source, middle, 0, head]
            values = received_ref[source, middle, 1, head]
            return one_step(head, keys, values, back, carry)

        accum, total, top = lax.fori_loop(1, steps, body, carry)
        out_ref[head] = (accum / total).astype(out_ref.dtype)


def attend(r_index, query, own_pair, received, q_prompt, q_where, k_prompt, k_where):
    heads, rows, width = query.shape
    steps = k_prompt.shape[0]
    flops = 4 * heads * rows * rows * width * steps
    vmem = pl.BlockSpec(memory_space=pltpu.VMEM)
    return pl.pallas_call(
        attend_kernel,
        out_shape=jax.ShapeDtypeStruct((heads, rows, width), jnp.bfloat16),
        in_specs=[pl.BlockSpec(memory_space=pltpu.SMEM)] + [vmem] * 7,
        out_specs=vmem,
        compiler_params=pltpu.CompilerParams(vmem_limit_bytes=48 * 1024 * 1024),
        cost_estimate=pl.CostEstimate(
            flops=flops,
            transcendentals=heads * rows * rows * steps,
            bytes_accessed=received.size * 2 + own_pair.size * 2 + query.size * 4,
        ),
    )(
        jnp.reshape(r_index, (1,)).astype(jnp.int32),
        query,
        own_pair,
        received,
        q_prompt.reshape(rows, 1).astype(jnp.int32),
        q_where.reshape(rows, 1).astype(jnp.int32),
        k_prompt.reshape(steps, 1, rows).astype(jnp.int32),
        k_where.reshape(steps, 1, rows).astype(jnp.int32),
    )


def on_device(tokens, lengths, w_query, w_key, w_value, w_out, w_gate, w_up, w_down):
    half_type = jnp.bfloat16
    dp = ("y", "r")
    mp = "mp"
    rows = tokens.shape[0]
    narrow = w_query.shape[1]
    shard_rows = w_query.shape[0]
    heads_dev = narrow // HEAD
    dp_index = lax.axis_index(dp)
    mp_index = lax.axis_index(mp)
    mp_size = lax.axis_size(mp)
    y_size = lax.axis_size("y")
    r_size = lax.axis_size("r")
    reach = lax.axis_size(dp) // 2

    down_rows = w_down.shape[0]
    per_mp = down_rows // mp_size
    units_shard = w_gate.shape[1]
    blocks = units_shard // down_rows

    def unit_pieces(w):
        pieces = w.astype(half_type).reshape(shard_rows, blocks, mp_size, per_mp)
        return jnp.transpose(pieces, (2, 0, 1, 3))

    outgoing = [
        unit_pieces(w_gate),
        unit_pieces(w_up),
        w_down.astype(half_type).reshape(mp_size, per_mp, narrow),
        jnp.broadcast_to(w_out.astype(half_type)[None], (mp_size,) + w_out.shape),
    ]
    flat = jnp.concatenate([p.reshape(mp_size, -1) for p in outgoing], axis=1)
    got = lax.all_to_all(flat, mp, 0, 0, tiled=True)
    kv_shard = jnp.concatenate([w.astype(half_type) for w in (w_key, w_value)], axis=1)
    got, kv_shard = lax.optimization_barrier((got, kv_shard))
    pieces = []
    at = 0
    for p in outgoing:
        size = p[0].size
        pieces.append(got[:, at : at + size].reshape(p.shape))
        at += size
    gate_got, up_got, down_got, out_got = pieces

    def unit_columns(got_w):
        return jnp.transpose(got_w, (1, 0, 2, 3)).reshape(shard_rows, mp_size * blocks * per_mp)

    gate_shard = unit_columns(gate_got)
    up_shard = unit_columns(up_got)
    down_shard = jnp.transpose(down_got, (1, 0, 2)).reshape(per_mp, mp_size * narrow)
    units = gate_shard.shape[1]
    rest_shard = jnp.concatenate(
        [w_query.astype(half_type), gate_shard, up_shard, down_shard.reshape(shard_rows, -1)], axis=1
    )

    out_full_rows = jnp.transpose(out_got, (1, 0, 2)).reshape(shard_rows, mp_size * narrow)
    swap = [(a * mp_size + b, b * mp_size + a) for a in range(y_size) for b in range(mp_size)]
    out_swapped = lax.ppermute(out_full_rows, ("y", mp), swap)
    server_out = gather_by_exchange(out_swapped, "r")

    kv_full = gather_by_exchange(kv_shard, dp)
    rest_full = lax.all_gather(rest_shard, dp, axis=0, tiled=True)

    normed = layer_norm(tokens).astype(half_type)
    joined_kv = jnp.dot(normed, kv_full, preferred_element_type=jnp.float32)
    q_prompt, q_offset, q_where = prompt_coords(dp_index * rows, rows, lengths)
    shaped = joined_kv.reshape(rows, 2, heads_dev, HEAD)
    keys = rotate(shaped[:, 0], q_offset).astype(half_type)
    values = shaped[:, 1].astype(half_type)
    own_pair = jnp.transpose(jnp.stack((keys, values)), (0, 2, 1, 3))
    plane = r_size
    back_one = shifted(own_pair, dp, plane)
    back_two = shifted(own_pair, dp, 2 * plane)
    own_first = dp_index * rows

    r_index = lax.axis_index("r")
    later = r_index < jnp.arange(plane)
    nearer = jnp.where(later[:, None, None, None, None], own_pair[None], back_two[None])
    payload = jnp.stack(
        (nearer, jnp.broadcast_to(back_one[None], (plane,) + back_one.shape)), axis=1
    )
    received = lax.all_to_all(payload, "r", 0, 0, tiled=True)
    q_full = rest_full[:, :narrow]
    server_gate = rest_full[:, narrow : narrow + units]
    server_up = rest_full[:, narrow + units : narrow + 2 * units]
    server_down = rest_full[:, narrow + 2 * units :].reshape(units, -1)
    received, q_full, server_gate, server_up, server_down = lax.optimization_barrier(
        (received, q_full, server_gate, server_up, server_down)
    )
    joined_q = jnp.dot(normed, q_full, preferred_element_type=jnp.float32)
    query = rotate(joined_q.reshape(rows, heads_dev, HEAD), q_offset).astype(half_type)
    query = jnp.transpose(query, (1, 0, 2))
    firsts = own_first - rows * jnp.arange(reach + 1)
    k_prompt, k_offset, k_where = jax.vmap(lambda first: prompt_coords(first, rows, lengths))(firsts)
    context = attend(r_index, query, own_pair, received, q_prompt, q_where, k_prompt, k_where)
    context = jnp.transpose(context, (1, 0, 2)).reshape(rows, narrow)

    partial_out = jnp.dot(context, server_out, preferred_element_type=jnp.float32)
    attended = scatter_sum(partial_out.astype(half_type), mp)
    slab = rows // mp_size
    own_tokens = lax.dynamic_slice_in_dim(tokens, mp_index * slab, slab, 0)
    mixed = (own_tokens.astype(jnp.float32) + attended).astype(half_type)
    normed_own = layer_norm(mixed).astype(half_type)
    normed_two = gather_by_exchange(normed_own, mp)

    gate = jnp.dot(normed_two, server_gate, preferred_element_type=jnp.float32)
    upper = jnp.dot(normed_two, server_up, preferred_element_type=jnp.float32)
    hidden = (jax.nn.silu(gate) * upper).astype(half_type)
    partial_down = jnp.dot(hidden, server_down, preferred_element_type=jnp.float32)
    share = scatter_sum(partial_down.astype(half_type), mp)
    return (mixed.astype(jnp.float32) + share).astype(half_type)


def solution(mesh):
    dp_size, mp_size = mesh.devices.shape
    y_size = mesh.devices.shape[0] // 8 if dp_size % 8 == 0 else 1
    fine = Mesh(mesh.devices.reshape(y_size, dp_size // y_size, mp_size), ("y", "r", "mp"))
    dp = ("y", "r")
    in_specs = (
        P(dp, None),
        P(),
        P(dp, "mp"),
        P(dp, "mp"),
        P(dp, "mp"),
        P(dp, "mp"),
        P(dp, "mp"),
        P(dp, "mp"),
        P(dp, "mp"),
    )
    out_specs = P(("y", "r", "mp"), None)
    return jax.shard_map(
        on_device, mesh=fine, in_specs=in_specs, out_specs=out_specs, check_vma=False
    )
```

```python
import jax
import jax.numpy as jnp
from jax import lax
from jax.sharding import Mesh, PartitionSpec as P
from jax.experimental import pallas as pl
from jax.experimental.pallas import tpu as pltpu

HEAD = 128


epsilon = 1e-05
theta_base = 10000.0


def shifted(value, axis, steps):
    count = lax.axis_size(axis)
    return lax.ppermute(value, axis, [(source, source + steps) for source in range(count - steps)])


def gather_by_exchange(value, axis):
    count = lax.axis_size(axis)
    copies = jnp.broadcast_to(value[None], (count,) + value.shape)
    got = lax.all_to_all(copies, axis, 0, 0, tiled=True)
    return got.reshape((count * value.shape[0],) + value.shape[1:])


def scatter_sum(value, axis):
    count = lax.axis_size(axis)
    pieces = value.reshape((count, value.shape[0] // count) + value.shape[1:])
    got = lax.all_to_all(pieces, axis, 0, 0, tiled=True)
    return jnp.sum(got.astype(jnp.float32), axis=0)


def layer_norm(rows):
    values = rows.astype(jnp.float32)
    centre = jnp.mean(values, axis=-1, keepdims=True)
    spread = jnp.mean(jnp.square(values - centre), axis=-1, keepdims=True)
    return (values - centre) * lax.rsqrt(spread + epsilon)


def prompt_coords(first, count, lengths):
    where = first + jnp.arange(count)
    ends = jnp.cumsum(lengths)
    passed = (ends[None, :] <= where[:, None]).astype(jnp.int32)
    prompt = jnp.sum(passed, axis=1)
    offset = where - jnp.sum(passed * lengths[None, :], axis=1)
    prompt = jnp.where(where < 0, -1, prompt)
    return (prompt, offset, where)


def rotate(values, offset):
    half = values.shape[-1] // 2
    freqs = jnp.power(theta_base, -jnp.arange(half, dtype=jnp.float32) * 2.0 / values.shape[-1])
    angles = offset.astype(jnp.float32)[:, None] * freqs[None, :]
    cosine = jnp.cos(angles)[:, None, :]
    sine = jnp.sin(angles)[:, None, :]
    first_half = values[..., :half]
    second_half = values[..., half:]
    return jnp.concatenate(
        [first_half * cosine - second_half * sine, second_half * cosine + first_half * sine],
        axis=-1,
    )


def attend_kernel(meta, query_ref, own_ref, received_ref, qp_ref, qw_ref, kp_ref, kw_ref, out_ref):
    r_index = meta[0]
    plane = received_ref.shape[0]
    steps = kp_ref.shape[0]
    heads = query_ref.shape[0]
    scale = 1.0 / query_ref.shape[-1] ** 0.5
    qp = qp_ref[...]
    qw = qw_ref[...]

    def one_step(head, keys, values, back, carry):
        accum, total, top = carry
        scores = lax.dot_general(
            query_ref[head], keys, (((1,), (1,)), ((), ())), preferred_element_type=jnp.float32
        ) * scale
        allowed = (qp == kp_ref[back]) & (kw_ref[back] <= qw)
        scores = jnp.where(allowed, scores, -jnp.inf)
        new_top = jnp.maximum(top, jnp.max(scores, axis=1, keepdims=True))
        fade = jnp.exp(top - new_top)
        weights = jnp.exp(scores - new_top)
        probs = weights.astype(jnp.bfloat16)
        product = jnp.dot(probs, values, preferred_element_type=jnp.float32)
        accum = accum * fade + product
        total = total * fade + jnp.sum(weights, axis=1, keepdims=True)
        return (accum, total, new_top)

    for head in range(heads):
        rows, width = query_ref.shape[1], query_ref.shape[2]
        carry = (
            jnp.zeros((rows, width), jnp.float32),
            jnp.zeros((rows, 1), jnp.float32),
            jnp.full((rows, 1), -jnp.inf, jnp.float32),
        )
        carry = one_step(head, own_ref[0, head], own_ref[1, head], 0, carry)

        def body(back, carry, head=head):
            source = lax.rem(r_index - back + 2 * plane, plane)
            middle = jnp.logical_and(back > r_index, back <= r_index + plane).astype(jnp.int32)
            keys = received_ref[source, middle, 0, head]
            values = received_ref[source, middle, 1, head]
            return one_step(head, keys, values, back, carry)

        accum, total, top = lax.fori_loop(1, steps, body, carry)
        out_ref[head] = (accum / total).astype(out_ref.dtype)


def attend(r_index, query, own_pair, received, q_prompt, q_where, k_prompt, k_where):
    heads, rows, width = query.shape
    steps = k_prompt.shape[0]
    flops = 4 * heads * rows * rows * width * steps
    vmem = pl.BlockSpec(memory_space=pltpu.VMEM)
    return pl.pallas_call(
        attend_kernel,
        out_shape=jax.ShapeDtypeStruct((heads, rows, width), jnp.bfloat16),
        in_specs=[pl.BlockSpec(memory_space=pltpu.SMEM)] + [vmem] * 7,
        out_specs=vmem,
        compiler_params=pltpu.CompilerParams(vmem_limit_bytes=48 * 1024 * 1024),
        cost_estimate=pl.CostEstimate(
            flops=flops,
            transcendentals=heads * rows * rows * steps,
            bytes_accessed=received.size * 2 + own_pair.size * 2 + query.size * 4,
        ),
    )(
        jnp.reshape(r_index, (1,)).astype(jnp.int32),
        query,
        own_pair,
        received,
        q_prompt.reshape(rows, 1).astype(jnp.int32),
        q_where.reshape(rows, 1).astype(jnp.int32),
        k_prompt.reshape(steps, 1, rows).astype(jnp.int32),
        k_where.reshape(steps, 1, rows).astype(jnp.int32),
    )


def on_device(tokens, lengths, w_query, w_key, w_value, w_out, w_gate, w_up, w_down):
    half_type = jnp.bfloat16
    dp = ("y", "r")
    mp = "mp"
    rows = tokens.shape[0]
    narrow = w_query.shape[1]
    shard_rows = w_query.shape[0]
    heads_dev = narrow // HEAD
    dp_index = lax.axis_index(dp)
    mp_index = lax.axis_index(mp)
    mp_size = lax.axis_size(mp)
    y_size = lax.axis_size("y")
    r_size = lax.axis_size("r")
    reach = lax.axis_size(dp) // 2

    down_rows = w_down.shape[0]
    per_mp = down_rows // mp_size
    units_shard = w_gate.shape[1]
    blocks = units_shard // down_rows

    def unit_pieces(w):
        pieces = w.astype(half_type).reshape(shard_rows, blocks, mp_size, per_mp)
        return jnp.transpose(pieces, (2, 0, 1, 3))

    outgoing = [
        unit_pieces(w_gate),
        unit_pieces(w_up),
        w_down.astype(half_type).reshape(mp_size, per_mp, narrow),
        jnp.broadcast_to(w_out.astype(half_type)[None], (mp_size,) + w_out.shape),
    ]
    flat = jnp.concatenate([p.reshape(mp_size, -1) for p in outgoing], axis=1)
    got = lax.all_to_all(flat, mp, 0, 0, tiled=True)
    kv_shard = jnp.concatenate([w.astype(half_type) for w in (w_key, w_value)], axis=1)
    got, kv_shard = lax.optimization_barrier((got, kv_shard))
    pieces = []
    at = 0
    for p in outgoing:
        size = p[0].size
        pieces.append(got[:, at : at + size].reshape(p.shape))
        at += size
    gate_got, up_got, down_got, out_got = pieces

    def unit_columns(got_w):
        return jnp.transpose(got_w, (1, 0, 2, 3)).reshape(shard_rows, mp_size * blocks * per_mp)

    gate_shard = unit_columns(gate_got)
    up_shard = unit_columns(up_got)
    down_shard = jnp.transpose(down_got, (1, 0, 2)).reshape(per_mp, mp_size * narrow)
    units = gate_shard.shape[1]
    rest_shard = jnp.concatenate(
        [w_query.astype(half_type), gate_shard, up_shard, down_shard.reshape(shard_rows, -1)], axis=1
    )

    out_full_rows = jnp.transpose(out_got, (1, 0, 2)).reshape(shard_rows, mp_size * narrow)
    swap = [(a * mp_size + b, b * mp_size + a) for a in range(y_size) for b in range(mp_size)]
    out_swapped = lax.ppermute(out_full_rows, ("y", mp), swap)
    server_out = gather_by_exchange(out_swapped, "r")

    kv_full = gather_by_exchange(kv_shard, dp)
    rest_full = lax.all_gather(rest_shard, dp, axis=0, tiled=True)

    normed = layer_norm(tokens).astype(half_type)
    joined_kv = jnp.dot(normed, kv_full, preferred_element_type=jnp.float32)
    q_prompt, q_offset, q_where = prompt_coords(dp_index * rows, rows, lengths)
    shaped = joined_kv.reshape(rows, 2, heads_dev, HEAD)
    keys = rotate(shaped[:, 0], q_offset).astype(half_type)
    values = shaped[:, 1].astype(half_type)
    own_pair = jnp.transpose(jnp.stack((keys, values)), (0, 2, 1, 3))
    plane = r_size
    back_one = shifted(own_pair, dp, plane)
    back_two = shifted(own_pair, dp, 2 * plane)
    own_first = dp_index * rows

    r_index = lax.axis_index("r")
    later = r_index < jnp.arange(plane)
    nearer = jnp.where(later[:, None, None, None, None], own_pair[None], back_two[None])
    payload = jnp.stack(
        (nearer, jnp.broadcast_to(back_one[None], (plane,) + back_one.shape)), axis=1
    )
    received = lax.all_to_all(payload, "r", 0, 0, tiled=True)
    received, rest_full = lax.optimization_barrier((received, rest_full))
    q_full = rest_full[:, :narrow]
    server_gate = rest_full[:, narrow : narrow + units]
    server_up = rest_full[:, narrow + units : narrow + 2 * units]
    server_down = rest_full[:, narrow + 2 * units :].reshape(units, -1)
    joined_q = jnp.dot(normed, q_full, preferred_element_type=jnp.float32)
    query = rotate(joined_q.reshape(rows, heads_dev, HEAD), q_offset).astype(half_type)
    query = jnp.transpose(query, (1, 0, 2))
    firsts = own_first - rows * jnp.arange(reach + 1)
    k_prompt, k_offset, k_where = jax.vmap(lambda first: prompt_coords(first, rows, lengths))(firsts)
    context = attend(r_index, query, own_pair, received, q_prompt, q_where, k_prompt, k_where)
    context = jnp.transpose(context, (1, 0, 2)).reshape(rows, narrow)

    partial_out = jnp.dot(context, server_out, preferred_element_type=jnp.float32)
    attended = scatter_sum(partial_out.astype(half_type), mp)
    slab = rows // mp_size
    own_tokens = lax.dynamic_slice_in_dim(tokens, mp_index * slab, slab, 0)
    mixed = (own_tokens.astype(jnp.float32) + attended).astype(half_type)
    normed_own = layer_norm(mixed).astype(half_type)
    normed_two = gather_by_exchange(normed_own, mp)

    gate = jnp.dot(normed_two, server_gate, preferred_element_type=jnp.float32)
    upper = jnp.dot(normed_two, server_up, preferred_element_type=jnp.float32)
    hidden = (jax.nn.silu(gate) * upper).astype(half_type)
    partial_down = jnp.dot(hidden, server_down, preferred_element_type=jnp.float32)
    share = scatter_sum(partial_down.astype(half_type), mp)
    return (mixed.astype(jnp.float32) + share).astype(half_type)


def solution(mesh):
    dp_size, mp_size = mesh.devices.shape
    y_size = mesh.devices.shape[0] // 8 if dp_size % 8 == 0 else 1
    fine = Mesh(mesh.devices.reshape(y_size, dp_size // y_size, mp_size), ("y", "r", "mp"))
    dp = ("y", "r")
    in_specs = (
        P(dp, None),
        P(),
        P(dp, "mp"),
        P(dp, "mp"),
        P(dp, "mp"),
        P(dp, "mp"),
        P(dp, "mp"),
        P(dp, "mp"),
        P(dp, "mp"),
    )
    out_specs = P(("y", "r", "mp"), None)
    return jax.shard_map(
        on_device, mesh=fine, in_specs=in_specs, out_specs=out_specs, check_vma=False
    )
```

```python
import jax
import jax.numpy as jnp
from jax import lax
from jax.sharding import Mesh, PartitionSpec as P
from jax.experimental import pallas as pl
from jax.experimental.pallas import tpu as pltpu

HEAD = 128


epsilon = 1e-05
theta_base = 10000.0


def shifted(value, axis, steps):
    count = lax.axis_size(axis)
    return lax.ppermute(value, axis, [(source, source + steps) for source in range(count - steps)])


def gather_by_exchange(value, axis):
    count = lax.axis_size(axis)
    copies = jnp.broadcast_to(value[None], (count,) + value.shape)
    got = lax.all_to_all(copies, axis, 0, 0, tiled=True)
    return got.reshape((count * value.shape[0],) + value.shape[1:])


def scatter_sum(value, axis):
    count = lax.axis_size(axis)
    pieces = value.reshape((count, value.shape[0] // count) + value.shape[1:])
    got = lax.all_to_all(pieces, axis, 0, 0, tiled=True)
    return jnp.sum(got.astype(jnp.float32), axis=0)


def layer_norm(rows):
    values = rows.astype(jnp.float32)
    centre = jnp.mean(values, axis=-1, keepdims=True)
    spread = jnp.mean(jnp.square(values - centre), axis=-1, keepdims=True)
    return (values - centre) * lax.rsqrt(spread + epsilon)


def prompt_coords(first, count, lengths):
    where = first + jnp.arange(count)
    ends = jnp.cumsum(lengths)
    passed = (ends[None, :] <= where[:, None]).astype(jnp.int32)
    prompt = jnp.sum(passed, axis=1)
    offset = where - jnp.sum(passed * lengths[None, :], axis=1)
    prompt = jnp.where(where < 0, -1, prompt)
    return (prompt, offset, where)


def rotate(values, offset):
    half = values.shape[-1] // 2
    freqs = jnp.power(theta_base, -jnp.arange(half, dtype=jnp.float32) * 2.0 / values.shape[-1])
    angles = offset.astype(jnp.float32)[:, None] * freqs[None, :]
    cosine = jnp.cos(angles)[:, None, :]
    sine = jnp.sin(angles)[:, None, :]
    first_half = values[..., :half]
    second_half = values[..., half:]
    return jnp.concatenate(
        [first_half * cosine - second_half * sine, second_half * cosine + first_half * sine],
        axis=-1,
    )


def attend_kernel(meta, query_ref, own_ref, received_ref, qp_ref, qw_ref, kp_ref, kw_ref, out_ref):
    r_index = meta[0]
    plane = received_ref.shape[0]
    steps = kp_ref.shape[0]
    heads = query_ref.shape[0]
    scale = 1.0 / query_ref.shape[-1] ** 0.5
    qp = qp_ref[...]
    qw = qw_ref[...]

    def one_step(head, keys, values, back, carry, masked=True):
        accum, total, top = carry
        scores = lax.dot_general(
            query_ref[head], keys, (((1,), (1,)), ((), ())), preferred_element_type=jnp.float32
        ) * scale
        if masked:
            allowed = (qp == kp_ref[back]) & (kw_ref[back] <= qw)
            scores = jnp.where(allowed, scores, -jnp.inf)
        new_top = jnp.maximum(top, jnp.max(scores, axis=1, keepdims=True))
        fade = jnp.exp(top - new_top)
        weights = jnp.exp(scores - new_top)
        probs = weights.astype(jnp.bfloat16)
        product = jnp.dot(probs, values, preferred_element_type=jnp.float32)
        accum = accum * fade + product
        total = total * fade + jnp.sum(weights, axis=1, keepdims=True)
        return (accum, total, new_top)

    for head in range(heads):
        rows, width = query_ref.shape[1], query_ref.shape[2]
        carry = (
            jnp.zeros((rows, width), jnp.float32),
            jnp.zeros((rows, 1), jnp.float32),
            jnp.full((rows, 1), -jnp.inf, jnp.float32),
        )
        carry = one_step(head, own_ref[0, head], own_ref[1, head], 0, carry)

        def body(back, carry, head=head):
            source = lax.rem(r_index - back + 2 * plane, plane)
            middle = jnp.logical_and(back > r_index, back <= r_index + plane).astype(jnp.int32)
            mode = meta[1 + back]

            def run(carry, masked):
                keys = received_ref[source, middle, 0, head]
                values = received_ref[source, middle, 1, head]
                return one_step(head, keys, values, back, carry, masked)

            return lax.cond(
                mode == 0,
                lambda carry: carry,
                lambda carry: lax.cond(
                    mode == 2, lambda c: run(c, False), lambda c: run(c, True), carry
                ),
                carry,
            )

        accum, total, top = lax.fori_loop(1, steps, body, carry)
        out_ref[head] = (accum / total).astype(out_ref.dtype)


def attend(r_index, query, own_pair, received, q_prompt, q_where, k_prompt, k_where):
    heads, rows, width = query.shape
    steps = k_prompt.shape[0]
    empty = k_prompt[:, -1] < q_prompt[0]
    full = (k_prompt[:, 0] == q_prompt[-1]) & (k_prompt[:, -1] == q_prompt[0])
    full = full & (jnp.arange(steps) > 0)
    mode = jnp.where(empty, 0, jnp.where(full, 2, 1)).astype(jnp.int32)
    flops = 4 * heads * rows * rows * width * steps
    vmem = pl.BlockSpec(memory_space=pltpu.VMEM)
    return pl.pallas_call(
        attend_kernel,
        out_shape=jax.ShapeDtypeStruct((heads, rows, width), jnp.bfloat16),
        in_specs=[pl.BlockSpec(memory_space=pltpu.SMEM)] + [vmem] * 7,
        out_specs=vmem,
        compiler_params=pltpu.CompilerParams(vmem_limit_bytes=48 * 1024 * 1024),
        cost_estimate=pl.CostEstimate(
            flops=flops,
            transcendentals=heads * rows * rows * steps,
            bytes_accessed=received.size * 2 + own_pair.size * 2 + query.size * 4,
        ),
    )(
        jnp.concatenate([jnp.reshape(r_index, (1,)).astype(jnp.int32), mode]),
        query,
        own_pair,
        received,
        q_prompt.reshape(rows, 1).astype(jnp.int32),
        q_where.reshape(rows, 1).astype(jnp.int32),
        k_prompt.reshape(steps, 1, rows).astype(jnp.int32),
        k_where.reshape(steps, 1, rows).astype(jnp.int32),
    )


def on_device(tokens, lengths, w_query, w_key, w_value, w_out, w_gate, w_up, w_down):
    half_type = jnp.bfloat16
    dp = ("y", "r")
    mp = "mp"
    rows = tokens.shape[0]
    narrow = w_query.shape[1]
    shard_rows = w_query.shape[0]
    heads_dev = narrow // HEAD
    dp_index = lax.axis_index(dp)
    mp_index = lax.axis_index(mp)
    mp_size = lax.axis_size(mp)
    y_size = lax.axis_size("y")
    r_size = lax.axis_size("r")
    reach = lax.axis_size(dp) // 2

    down_rows = w_down.shape[0]
    per_mp = down_rows // mp_size
    units_shard = w_gate.shape[1]
    blocks = units_shard // down_rows

    def unit_pieces(w):
        pieces = w.astype(half_type).reshape(shard_rows, blocks, mp_size, per_mp)
        return jnp.transpose(pieces, (2, 0, 1, 3))

    outgoing = [
        unit_pieces(w_gate),
        unit_pieces(w_up),
        w_down.astype(half_type).reshape(mp_size, per_mp, narrow),
        jnp.broadcast_to(w_out.astype(half_type)[None], (mp_size,) + w_out.shape),
    ]
    flat = jnp.concatenate([p.reshape(mp_size, -1) for p in outgoing], axis=1)
    got = lax.all_to_all(flat, mp, 0, 0, tiled=True)
    kv_shard = jnp.concatenate([w.astype(half_type) for w in (w_key, w_value)], axis=1)
    got, kv_shard = lax.optimization_barrier((got, kv_shard))
    pieces = []
    at = 0
    for p in outgoing:
        size = p[0].size
        pieces.append(got[:, at : at + size].reshape(p.shape))
        at += size
    gate_got, up_got, down_got, out_got = pieces

    def unit_columns(got_w):
        return jnp.transpose(got_w, (1, 0, 2, 3)).reshape(shard_rows, mp_size * blocks * per_mp)

    gate_shard = unit_columns(gate_got)
    up_shard = unit_columns(up_got)
    down_shard = jnp.transpose(down_got, (1, 0, 2)).reshape(per_mp, mp_size * narrow)
    units = gate_shard.shape[1]
    rest_shard = jnp.concatenate(
        [w_query.astype(half_type), gate_shard, up_shard, down_shard.reshape(shard_rows, -1)], axis=1
    )

    out_full_rows = jnp.transpose(out_got, (1, 0, 2)).reshape(shard_rows, mp_size * narrow)
    swap = [(a * mp_size + b, b * mp_size + a) for a in range(y_size) for b in range(mp_size)]
    out_swapped = lax.ppermute(out_full_rows, ("y", mp), swap)
    server_out = gather_by_exchange(out_swapped, "r")

    kv_full = gather_by_exchange(kv_shard, dp)
    rest_full = lax.all_gather(rest_shard, dp, axis=0, tiled=True)

    normed = layer_norm(tokens).astype(half_type)
    joined_kv = jnp.dot(normed, kv_full, preferred_element_type=jnp.float32)
    q_prompt, q_offset, q_where = prompt_coords(dp_index * rows, rows, lengths)
    shaped = joined_kv.reshape(rows, 2, heads_dev, HEAD)
    keys = rotate(shaped[:, 0], q_offset).astype(half_type)
    values = shaped[:, 1].astype(half_type)
    own_pair = jnp.transpose(jnp.stack((keys, values)), (0, 2, 1, 3))
    plane = r_size
    back_one = shifted(own_pair, dp, plane)
    back_two = shifted(own_pair, dp, 2 * plane)
    own_first = dp_index * rows

    r_index = lax.axis_index("r")
    later = r_index < jnp.arange(plane)
    nearer = jnp.where(later[:, None, None, None, None], own_pair[None], back_two[None])
    payload = jnp.stack(
        (nearer, jnp.broadcast_to(back_one[None], (plane,) + back_one.shape)), axis=1
    )
    received = lax.all_to_all(payload, "r", 0, 0, tiled=True)
    received, rest_full = lax.optimization_barrier((received, rest_full))
    q_full = rest_full[:, :narrow]
    server_gate = rest_full[:, narrow : narrow + units]
    server_up = rest_full[:, narrow + units : narrow + 2 * units]
    server_down = rest_full[:, narrow + 2 * units :].reshape(units, -1)
    joined_q = jnp.dot(normed, q_full, preferred_element_type=jnp.float32)
    query = rotate(joined_q.reshape(rows, heads_dev, HEAD), q_offset).astype(half_type)
    query = jnp.transpose(query, (1, 0, 2))
    firsts = own_first - rows * jnp.arange(reach + 1)
    k_prompt, k_offset, k_where = jax.vmap(lambda first: prompt_coords(first, rows, lengths))(firsts)
    context = attend(r_index, query, own_pair, received, q_prompt, q_where, k_prompt, k_where)
    context = jnp.transpose(context, (1, 0, 2)).reshape(rows, narrow)

    partial_out = jnp.dot(context, server_out, preferred_element_type=jnp.float32)
    attended = scatter_sum(partial_out.astype(half_type), mp)
    slab = rows // mp_size
    own_tokens = lax.dynamic_slice_in_dim(tokens, mp_index * slab, slab, 0)
    mixed = (own_tokens.astype(jnp.float32) + attended).astype(half_type)
    normed_own = layer_norm(mixed).astype(half_type)
    normed_two = gather_by_exchange(normed_own, mp)

    gate = jnp.dot(normed_two, server_gate, preferred_element_type=jnp.float32)
    upper = jnp.dot(normed_two, server_up, preferred_element_type=jnp.float32)
    hidden = (jax.nn.silu(gate) * upper).astype(half_type)
    partial_down = jnp.dot(hidden, server_down, preferred_element_type=jnp.float32)
    share = scatter_sum(partial_down.astype(half_type), mp)
    return (mixed.astype(jnp.float32) + share).astype(half_type)


def solution(mesh):
    dp_size, mp_size = mesh.devices.shape
    y_size = mesh.devices.shape[0] // 8 if dp_size % 8 == 0 else 1
    fine = Mesh(mesh.devices.reshape(y_size, dp_size // y_size, mp_size), ("y", "r", "mp"))
    dp = ("y", "r")
    in_specs = (
        P(dp, None),
        P(),
        P(dp, "mp"),
        P(dp, "mp"),
        P(dp, "mp"),
        P(dp, "mp"),
        P(dp, "mp"),
        P(dp, "mp"),
        P(dp, "mp"),
    )
    out_specs = P(("y", "r", "mp"), None)
    return jax.shard_map(
        on_device, mesh=fine, in_specs=in_specs, out_specs=out_specs, check_vma=False
    )
```

```python
import jax
import jax.numpy as jnp
from jax import lax
from jax.sharding import Mesh, PartitionSpec as P
from jax.experimental import pallas as pl
from jax.experimental.pallas import tpu as pltpu

HEAD = 128


epsilon = 1e-05
theta_base = 10000.0


def shifted(value, axis, steps):
    count = lax.axis_size(axis)
    return lax.ppermute(value, axis, [(source, source + steps) for source in range(count - steps)])


def gather_by_exchange(value, axis):
    count = lax.axis_size(axis)
    copies = jnp.broadcast_to(value[None], (count,) + value.shape)
    got = lax.all_to_all(copies, axis, 0, 0, tiled=True)
    return got.reshape((count * value.shape[0],) + value.shape[1:])


def scatter_sum(value, axis):
    count = lax.axis_size(axis)
    pieces = value.reshape((count, value.shape[0] // count) + value.shape[1:])
    got = lax.all_to_all(pieces, axis, 0, 0, tiled=True)
    return jnp.sum(got.astype(jnp.float32), axis=0)


def layer_norm(rows):
    values = rows.astype(jnp.float32)
    centre = jnp.mean(values, axis=-1, keepdims=True)
    spread = jnp.mean(jnp.square(values - centre), axis=-1, keepdims=True)
    return (values - centre) * lax.rsqrt(spread + epsilon)


def prompt_coords(first, count, lengths):
    where = first + jnp.arange(count)
    ends = jnp.cumsum(lengths)
    passed = (ends[None, :] <= where[:, None]).astype(jnp.int32)
    prompt = jnp.sum(passed, axis=1)
    offset = where - jnp.sum(passed * lengths[None, :], axis=1)
    prompt = jnp.where(where < 0, -1, prompt)
    return (prompt, offset, where)


def rotate(values, offset):
    half = values.shape[-1] // 2
    freqs = jnp.power(theta_base, -jnp.arange(half, dtype=jnp.float32) * 2.0 / values.shape[-1])
    angles = offset.astype(jnp.float32)[:, None] * freqs[None, :]
    cosine = jnp.cos(angles)[:, None, :]
    sine = jnp.sin(angles)[:, None, :]
    first_half = values[..., :half]
    second_half = values[..., half:]
    return jnp.concatenate(
        [first_half * cosine - second_half * sine, second_half * cosine + first_half * sine],
        axis=-1,
    )


def attend_kernel(meta, query_ref, own_ref, received_ref, qp_ref, qw_ref, kp_ref, kw_ref, out_ref):
    r_index = meta[0]
    plane = received_ref.shape[0]
    steps = kp_ref.shape[0]
    heads = query_ref.shape[0]
    scale = 1.0 / query_ref.shape[-1] ** 0.5
    qp = qp_ref[...]
    qw = qw_ref[...]

    def one_step(head, keys, values, back, carry):
        accum, total, top = carry
        scores = lax.dot_general(
            query_ref[head], keys, (((1,), (1,)), ((), ())), preferred_element_type=jnp.float32
        ) * scale
        allowed = (qp == kp_ref[back]) & (kw_ref[back] <= qw)
        scores = jnp.where(allowed, scores, -jnp.inf)
        new_top = jnp.maximum(top, jnp.max(scores, axis=1, keepdims=True))
        fade = jnp.exp(top - new_top)
        weights = jnp.exp(scores - new_top)
        probs = weights.astype(jnp.bfloat16)
        product = jnp.dot(probs, values, preferred_element_type=jnp.float32)
        accum = accum * fade + product
        total = total * fade + jnp.sum(weights, axis=1, keepdims=True)
        return (accum, total, new_top)

    rows, width = query_ref.shape[1], query_ref.shape[2]
    carries = []
    for head in range(heads):
        carry = (
            jnp.zeros((rows, width), jnp.float32),
            jnp.zeros((rows, 1), jnp.float32),
            jnp.full((rows, 1), -jnp.inf, jnp.float32),
        )
        carries.append(one_step(head, own_ref[0, head], own_ref[1, head], 0, carry))

    def body(back, carries):
        source = lax.rem(r_index - back + 2 * plane, plane)
        middle = jnp.logical_and(back > r_index, back <= r_index + plane).astype(jnp.int32)
        return tuple(
            one_step(
                head,
                received_ref[source, middle, 0, head],
                received_ref[source, middle, 1, head],
                back,
                carries[head],
            )
            for head in range(heads)
        )

    carries = lax.fori_loop(1, steps, body, tuple(carries))
    for head in range(heads):
        accum, total, top = carries[head]
        out_ref[head] = (accum / total).astype(out_ref.dtype)


def attend(r_index, query, own_pair, received, q_prompt, q_where, k_prompt, k_where):
    heads, rows, width = query.shape
    steps = k_prompt.shape[0]
    flops = 4 * heads * rows * rows * width * steps
    vmem = pl.BlockSpec(memory_space=pltpu.VMEM)
    return pl.pallas_call(
        attend_kernel,
        out_shape=jax.ShapeDtypeStruct((heads, rows, width), jnp.bfloat16),
        in_specs=[pl.BlockSpec(memory_space=pltpu.SMEM)] + [vmem] * 7,
        out_specs=vmem,
        compiler_params=pltpu.CompilerParams(vmem_limit_bytes=48 * 1024 * 1024),
        cost_estimate=pl.CostEstimate(
            flops=flops,
            transcendentals=heads * rows * rows * steps,
            bytes_accessed=received.size * 2 + own_pair.size * 2 + query.size * 4,
        ),
    )(
        jnp.reshape(r_index, (1,)).astype(jnp.int32),
        query,
        own_pair,
        received,
        q_prompt.reshape(rows, 1).astype(jnp.int32),
        q_where.reshape(rows, 1).astype(jnp.int32),
        k_prompt.reshape(steps, 1, rows).astype(jnp.int32),
        k_where.reshape(steps, 1, rows).astype(jnp.int32),
    )


def on_device(tokens, lengths, w_query, w_key, w_value, w_out, w_gate, w_up, w_down):
    half_type = jnp.bfloat16
    dp = ("y", "r")
    mp = "mp"
    rows = tokens.shape[0]
    narrow = w_query.shape[1]
    shard_rows = w_query.shape[0]
    heads_dev = narrow // HEAD
    dp_index = lax.axis_index(dp)
    mp_index = lax.axis_index(mp)
    mp_size = lax.axis_size(mp)
    y_size = lax.axis_size("y")
    r_size = lax.axis_size("r")
    reach = lax.axis_size(dp) // 2

    down_rows = w_down.shape[0]
    per_mp = down_rows // mp_size
    units_shard = w_gate.shape[1]
    blocks = units_shard // down_rows

    def unit_pieces(w):
        pieces = w.astype(half_type).reshape(shard_rows, blocks, mp_size, per_mp)
        return jnp.transpose(pieces, (2, 0, 1, 3))

    outgoing = [
        unit_pieces(w_gate),
        unit_pieces(w_up),
        w_down.astype(half_type).reshape(mp_size, per_mp, narrow),
        jnp.broadcast_to(w_out.astype(half_type)[None], (mp_size,) + w_out.shape),
    ]
    flat = jnp.concatenate([p.reshape(mp_size, -1) for p in outgoing], axis=1)
    got = lax.all_to_all(flat, mp, 0, 0, tiled=True)
    kv_shard = jnp.concatenate([w.astype(half_type) for w in (w_key, w_value)], axis=1)
    got, kv_shard = lax.optimization_barrier((got, kv_shard))
    pieces = []
    at = 0
    for p in outgoing:
        size = p[0].size
        pieces.append(got[:, at : at + size].reshape(p.shape))
        at += size
    gate_got, up_got, down_got, out_got = pieces

    def unit_columns(got_w):
        return jnp.transpose(got_w, (1, 0, 2, 3)).reshape(shard_rows, mp_size * blocks * per_mp)

    gate_shard = unit_columns(gate_got)
    up_shard = unit_columns(up_got)
    down_shard = jnp.transpose(down_got, (1, 0, 2)).reshape(per_mp, mp_size * narrow)
    units = gate_shard.shape[1]
    rest_shard = jnp.concatenate(
        [w_query.astype(half_type), gate_shard, up_shard, down_shard.reshape(shard_rows, -1)], axis=1
    )

    out_full_rows = jnp.transpose(out_got, (1, 0, 2)).reshape(shard_rows, mp_size * narrow)
    swap = [(a * mp_size + b, b * mp_size + a) for a in range(y_size) for b in range(mp_size)]
    out_swapped = lax.ppermute(out_full_rows, ("y", mp), swap)
    server_out = gather_by_exchange(out_swapped, "r")

    kv_full = gather_by_exchange(kv_shard, dp)
    rest_full = lax.all_gather(rest_shard, dp, axis=0, tiled=True)

    normed = layer_norm(tokens).astype(half_type)
    joined_kv = jnp.dot(normed, kv_full, preferred_element_type=jnp.float32)
    q_prompt, q_offset, q_where = prompt_coords(dp_index * rows, rows, lengths)
    shaped = joined_kv.reshape(rows, 2, heads_dev, HEAD)
    keys = rotate(shaped[:, 0], q_offset).astype(half_type)
    values = shaped[:, 1].astype(half_type)
    own_pair = jnp.transpose(jnp.stack((keys, values)), (0, 2, 1, 3))
    plane = r_size
    back_one = shifted(own_pair, dp, plane)
    back_two = shifted(own_pair, dp, 2 * plane)
    own_first = dp_index * rows

    r_index = lax.axis_index("r")
    later = r_index < jnp.arange(plane)
    nearer = jnp.where(later[:, None, None, None, None], own_pair[None], back_two[None])
    payload = jnp.stack(
        (nearer, jnp.broadcast_to(back_one[None], (plane,) + back_one.shape)), axis=1
    )
    received = lax.all_to_all(payload, "r", 0, 0, tiled=True)
    received, rest_full = lax.optimization_barrier((received, rest_full))
    q_full = rest_full[:, :narrow]
    server_gate = rest_full[:, narrow : narrow + units]
    server_up = rest_full[:, narrow + units : narrow + 2 * units]
    server_down = rest_full[:, narrow + 2 * units :].reshape(units, -1)
    joined_q = jnp.dot(normed, q_full, preferred_element_type=jnp.float32)
    query = rotate(joined_q.reshape(rows, heads_dev, HEAD), q_offset).astype(half_type)
    query = jnp.transpose(query, (1, 0, 2))
    firsts = own_first - rows * jnp.arange(reach + 1)
    k_prompt, k_offset, k_where = jax.vmap(lambda first: prompt_coords(first, rows, lengths))(firsts)
    context = attend(r_index, query, own_pair, received, q_prompt, q_where, k_prompt, k_where)
    context = jnp.transpose(context, (1, 0, 2)).reshape(rows, narrow)

    partial_out = jnp.dot(context, server_out, preferred_element_type=jnp.float32)
    attended = scatter_sum(partial_out.astype(half_type), mp)
    slab = rows // mp_size
    own_tokens = lax.dynamic_slice_in_dim(tokens, mp_index * slab, slab, 0)
    mixed = (own_tokens.astype(jnp.float32) + attended).astype(half_type)
    normed_own = layer_norm(mixed).astype(half_type)
    normed_two = gather_by_exchange(normed_own, mp)

    gate = jnp.dot(normed_two, server_gate, preferred_element_type=jnp.float32)
    upper = jnp.dot(normed_two, server_up, preferred_element_type=jnp.float32)
    hidden = (jax.nn.silu(gate) * upper).astype(half_type)
    partial_down = jnp.dot(hidden, server_down, preferred_element_type=jnp.float32)
    share = scatter_sum(partial_down.astype(half_type), mp)
    return (mixed.astype(jnp.float32) + share).astype(half_type)


def solution(mesh):
    dp_size, mp_size = mesh.devices.shape
    y_size = mesh.devices.shape[0] // 8 if dp_size % 8 == 0 else 1
    fine = Mesh(mesh.devices.reshape(y_size, dp_size // y_size, mp_size), ("y", "r", "mp"))
    dp = ("y", "r")
    in_specs = (
        P(dp, None),
        P(),
        P(dp, "mp"),
        P(dp, "mp"),
        P(dp, "mp"),
        P(dp, "mp"),
        P(dp, "mp"),
        P(dp, "mp"),
        P(dp, "mp"),
    )
    out_specs = P(("y", "r", "mp"), None)
    return jax.shard_map(
        on_device, mesh=fine, in_specs=in_specs, out_specs=out_specs, check_vma=False
    )
```

```python
import jax
import jax.numpy as jnp
from jax import lax
from jax.sharding import Mesh, PartitionSpec as P
from jax.experimental import pallas as pl
from jax.experimental.pallas import tpu as pltpu

HEAD = 128


epsilon = 1e-05
theta_base = 10000.0


def shifted(value, axis, steps):
    count = lax.axis_size(axis)
    return lax.ppermute(value, axis, [(source, source + steps) for source in range(count - steps)])


def gather_by_exchange(value, axis):
    count = lax.axis_size(axis)
    copies = jnp.broadcast_to(value[None], (count,) + value.shape)
    got = lax.all_to_all(copies, axis, 0, 0, tiled=True)
    return got.reshape((count * value.shape[0],) + value.shape[1:])


def scatter_sum(value, axis):
    count = lax.axis_size(axis)
    pieces = value.reshape((count, value.shape[0] // count) + value.shape[1:])
    got = lax.all_to_all(pieces, axis, 0, 0, tiled=True)
    return jnp.sum(got.astype(jnp.float32), axis=0)


def layer_norm(rows):
    values = rows.astype(jnp.float32)
    centre = jnp.mean(values, axis=-1, keepdims=True)
    spread = jnp.mean(jnp.square(values - centre), axis=-1, keepdims=True)
    return (values - centre) * lax.rsqrt(spread + epsilon)


def prompt_coords(first, count, lengths):
    where = first + jnp.arange(count)
    ends = jnp.cumsum(lengths)
    passed = (ends[None, :] <= where[:, None]).astype(jnp.int32)
    prompt = jnp.sum(passed, axis=1)
    offset = where - jnp.sum(passed * lengths[None, :], axis=1)
    prompt = jnp.where(where < 0, -1, prompt)
    return (prompt, offset, where)


def rotate(values, offset):
    half = values.shape[-1] // 2
    freqs = jnp.power(theta_base, -jnp.arange(half, dtype=jnp.float32) * 2.0 / values.shape[-1])
    angles = offset.astype(jnp.float32)[:, None] * freqs[None, :]
    cosine = jnp.cos(angles)[:, None, :]
    sine = jnp.sin(angles)[:, None, :]
    first_half = values[..., :half]
    second_half = values[..., half:]
    return jnp.concatenate(
        [first_half * cosine - second_half * sine, second_half * cosine + first_half * sine],
        axis=-1,
    )


def attend_kernel(meta, query_ref, own_ref, received_ref, qp_ref, qw_ref, kp_ref, kw_ref, out_ref):
    r_index = meta[0]
    plane = received_ref.shape[0]
    steps = kp_ref.shape[0]
    heads = query_ref.shape[0]
    scale = 1.0 / query_ref.shape[-1] ** 0.5
    qp = qp_ref[...]
    qw = qw_ref[...]

    def one_step(head, keys, values, back, carry):
        accum, total, top = carry
        scores = lax.dot_general(
            query_ref[head], keys, (((1,), (1,)), ((), ())), preferred_element_type=jnp.float32
        ) * scale
        allowed = (qp == kp_ref[back]) & (kw_ref[back] <= qw)
        scores = jnp.where(allowed, scores, -jnp.inf)
        new_top = jnp.maximum(top, jnp.max(scores, axis=1, keepdims=True))
        fade = jnp.exp(top - new_top)
        weights = jnp.exp(scores - new_top)
        probs = weights.astype(jnp.bfloat16)
        product = jnp.dot(probs, values, preferred_element_type=jnp.float32)
        accum = accum * fade + product
        total = total * fade + jnp.sum(weights, axis=1, keepdims=True)
        return (accum, total, new_top)

    rows, width = query_ref.shape[1], query_ref.shape[2]
    carries = []
    for head in range(heads):
        carry = (
            jnp.zeros((rows, width), jnp.float32),
            jnp.zeros((rows, 1), jnp.float32),
            jnp.full((rows, 1), -jnp.inf, jnp.float32),
        )
        carries.append(one_step(head, own_ref[0, head], own_ref[1, head], 0, carry))

    def body(back, carries):
        source = lax.rem(r_index - back + 2 * plane, plane)
        middle = jnp.logical_and(back > r_index, back <= r_index + plane).astype(jnp.int32)
        return tuple(
            one_step(
                head,
                received_ref[source, middle, 0, head],
                received_ref[source, middle, 1, head],
                back,
                carries[head],
            )
            for head in range(heads)
        )

    carries = lax.fori_loop(1, steps, body, tuple(carries))
    for head in range(heads):
        accum, total, top = carries[head]
        out_ref[head] = (accum / total).astype(out_ref.dtype)


def attend(r_index, query, own_pair, received, q_prompt, q_where, k_prompt, k_where):
    heads, rows, width = query.shape
    steps = k_prompt.shape[0]
    flops = 4 * heads * rows * rows * width * steps
    vmem = pl.BlockSpec(memory_space=pltpu.VMEM)
    return pl.pallas_call(
        attend_kernel,
        out_shape=jax.ShapeDtypeStruct((heads, rows, width), jnp.bfloat16),
        in_specs=[pl.BlockSpec(memory_space=pltpu.SMEM)] + [vmem] * 7,
        out_specs=vmem,
        compiler_params=pltpu.CompilerParams(vmem_limit_bytes=48 * 1024 * 1024),
        cost_estimate=pl.CostEstimate(
            flops=flops,
            transcendentals=heads * rows * rows * steps,
            bytes_accessed=received.size * 2 + own_pair.size * 2 + query.size * 4,
        ),
    )(
        jnp.reshape(r_index, (1,)).astype(jnp.int32),
        query,
        own_pair,
        received,
        q_prompt.reshape(rows, 1).astype(jnp.int32),
        q_where.reshape(rows, 1).astype(jnp.int32),
        k_prompt.reshape(steps, 1, rows).astype(jnp.int32),
        k_where.reshape(steps, 1, rows).astype(jnp.int32),
    )


def on_device(tokens, lengths, w_query, w_key, w_value, w_out, w_gate, w_up, w_down):
    half_type = jnp.bfloat16
    dp = ("y", "r")
    mp = "mp"
    rows = tokens.shape[0]
    narrow = w_query.shape[1]
    shard_rows = w_query.shape[0]
    heads_dev = narrow // HEAD
    dp_index = lax.axis_index(dp)
    mp_index = lax.axis_index(mp)
    mp_size = lax.axis_size(mp)
    y_size = lax.axis_size("y")
    r_size = lax.axis_size("r")
    reach = lax.axis_size(dp) // 2

    down_rows = w_down.shape[0]
    per_mp = down_rows // mp_size
    units_shard = w_gate.shape[1]
    blocks = units_shard // down_rows

    def unit_pieces(w):
        pieces = w.astype(half_type).reshape(shard_rows, blocks, mp_size, per_mp)
        return jnp.transpose(pieces, (2, 0, 1, 3))

    outgoing = [
        unit_pieces(w_gate),
        unit_pieces(w_up),
        w_down.astype(half_type).reshape(mp_size, per_mp, narrow),
        jnp.broadcast_to(w_out.astype(half_type)[None], (mp_size,) + w_out.shape),
    ]
    flat = jnp.concatenate([p.reshape(mp_size, -1) for p in outgoing], axis=1)
    got = lax.all_to_all(flat, mp, 0, 0, tiled=True)
    kv_shard = jnp.concatenate([w.astype(half_type) for w in (w_key, w_value)], axis=1)
    got, kv_shard = lax.optimization_barrier((got, kv_shard))
    pieces = []
    at = 0
    for p in outgoing:
        size = p[0].size
        pieces.append(got[:, at : at + size].reshape(p.shape))
        at += size
    gate_got, up_got, down_got, out_got = pieces

    def unit_columns(got_w):
        return jnp.transpose(got_w, (1, 0, 2, 3)).reshape(shard_rows, mp_size * blocks * per_mp)

    gate_shard = unit_columns(gate_got)
    up_shard = unit_columns(up_got)
    down_shard = jnp.transpose(down_got, (1, 0, 2)).reshape(per_mp, mp_size * narrow)
    units = gate_shard.shape[1]
    rest_shard = jnp.concatenate(
        [w_query.astype(half_type), gate_shard, up_shard, down_shard.reshape(shard_rows, -1)], axis=1
    )

    out_full_rows = jnp.transpose(out_got, (1, 0, 2)).reshape(shard_rows, mp_size * narrow)
    swap = [(a * mp_size + b, b * mp_size + a) for a in range(y_size) for b in range(mp_size)]
    out_swapped = lax.ppermute(out_full_rows, ("y", mp), swap)
    server_out = gather_by_exchange(out_swapped, "r")

    kv_full = gather_by_exchange(kv_shard, dp)
    rest_full = lax.all_gather(rest_shard, dp, axis=0, tiled=True)

    normed = layer_norm(tokens).astype(half_type)
    joined_kv = jnp.dot(normed, kv_full, preferred_element_type=jnp.float32)
    q_prompt, q_offset, q_where = prompt_coords(dp_index * rows, rows, lengths)
    shaped = joined_kv.reshape(rows, 2, heads_dev, HEAD)
    keys = rotate(shaped[:, 0], q_offset).astype(half_type)
    values = shaped[:, 1].astype(half_type)
    own_pair = jnp.transpose(jnp.stack((keys, values)), (0, 2, 1, 3))
    plane = r_size
    back_one = shifted(own_pair, dp, plane)
    back_two = shifted(own_pair, dp, 2 * plane)
    own_first = dp_index * rows

    r_index = lax.axis_index("r")
    later = r_index < jnp.arange(plane)
    first_slot = (jnp.arange(2) == 0)[None, :]
    pick_own = (later[:, None] & first_slot)[:, :, None, None, None, None]
    pick_two = (jnp.logical_not(later)[:, None] & first_slot)[:, :, None, None, None, None]
    payload = jnp.where(
        pick_own, own_pair[None, None], jnp.where(pick_two, back_two[None, None], back_one[None, None])
    )
    received = lax.all_to_all(payload, "r", 0, 0, tiled=True)
    received, rest_full = lax.optimization_barrier((received, rest_full))
    q_full = rest_full[:, :narrow]
    server_gate = rest_full[:, narrow : narrow + units]
    server_up = rest_full[:, narrow + units : narrow + 2 * units]
    server_down = rest_full[:, narrow + 2 * units :].reshape(units, -1)
    joined_q = jnp.dot(normed, q_full, preferred_element_type=jnp.float32)
    query = rotate(joined_q.reshape(rows, heads_dev, HEAD), q_offset).astype(half_type)
    query = jnp.transpose(query, (1, 0, 2))
    firsts = own_first - rows * jnp.arange(reach + 1)
    k_prompt, k_offset, k_where = jax.vmap(lambda first: prompt_coords(first, rows, lengths))(firsts)
    context = attend(r_index, query, own_pair, received, q_prompt, q_where, k_prompt, k_where)
    context = jnp.transpose(context, (1, 0, 2)).reshape(rows, narrow)

    partial_out = jnp.dot(context, server_out, preferred_element_type=jnp.float32)
    attended = scatter_sum(partial_out.astype(half_type), mp)
    slab = rows // mp_size
    own_tokens = lax.dynamic_slice_in_dim(tokens, mp_index * slab, slab, 0)
    mixed = (own_tokens.astype(jnp.float32) + attended).astype(half_type)
    normed_own = layer_norm(mixed).astype(half_type)
    normed_two = gather_by_exchange(normed_own, mp)

    gate = jnp.dot(normed_two, server_gate, preferred_element_type=jnp.float32)
    upper = jnp.dot(normed_two, server_up, preferred_element_type=jnp.float32)
    hidden = (jax.nn.silu(gate) * upper).astype(half_type)
    partial_down = jnp.dot(hidden, server_down, preferred_element_type=jnp.float32)
    share = scatter_sum(partial_down.astype(half_type), mp)
    return (mixed.astype(jnp.float32) + share).astype(half_type)


def solution(mesh):
    dp_size, mp_size = mesh.devices.shape
    y_size = mesh.devices.shape[0] // 8 if dp_size % 8 == 0 else 1
    fine = Mesh(mesh.devices.reshape(y_size, dp_size // y_size, mp_size), ("y", "r", "mp"))
    dp = ("y", "r")
    in_specs = (
        P(dp, None),
        P(),
        P(dp, "mp"),
        P(dp, "mp"),
        P(dp, "mp"),
        P(dp, "mp"),
        P(dp, "mp"),
        P(dp, "mp"),
        P(dp, "mp"),
    )
    out_specs = P(("y", "r", "mp"), None)
    return jax.shard_map(
        on_device, mesh=fine, in_specs=in_specs, out_specs=out_specs, check_vma=False
    )
```

```python
import jax
import jax.numpy as jnp
from jax import lax
from jax.sharding import Mesh, PartitionSpec as P
from jax.experimental import pallas as pl
from jax.experimental.pallas import tpu as pltpu

HEAD = 128


epsilon = 1e-05
theta_base = 10000.0


def shifted(value, axis, steps):
    count = lax.axis_size(axis)
    return lax.ppermute(value, axis, [(source, source + steps) for source in range(count - steps)])


def gather_by_exchange(value, axis):
    count = lax.axis_size(axis)
    copies = jnp.broadcast_to(value[None], (count,) + value.shape)
    got = lax.all_to_all(copies, axis, 0, 0, tiled=True)
    return got.reshape((count * value.shape[0],) + value.shape[1:])


def scatter_sum(value, axis):
    count = lax.axis_size(axis)
    pieces = value.reshape((count, value.shape[0] // count) + value.shape[1:])
    got = lax.all_to_all(pieces, axis, 0, 0, tiled=True)
    return jnp.sum(got.astype(jnp.float32), axis=0)


def layer_norm(rows):
    values = rows.astype(jnp.float32)
    centre = jnp.mean(values, axis=-1, keepdims=True)
    spread = jnp.mean(jnp.square(values - centre), axis=-1, keepdims=True)
    return (values - centre) * lax.rsqrt(spread + epsilon)


def prompt_coords(first, count, lengths):
    where = first + jnp.arange(count)
    ends = jnp.cumsum(lengths)
    passed = (ends[None, :] <= where[:, None]).astype(jnp.int32)
    prompt = jnp.sum(passed, axis=1)
    offset = where - jnp.sum(passed * lengths[None, :], axis=1)
    prompt = jnp.where(where < 0, -1, prompt)
    return (prompt, offset, where)


def rotate(values, offset):
    half = values.shape[-1] // 2
    freqs = jnp.power(theta_base, -jnp.arange(half, dtype=jnp.float32) * 2.0 / values.shape[-1])
    angles = offset.astype(jnp.float32)[:, None] * freqs[None, :]
    cosine = jnp.cos(angles)[:, None, :]
    sine = jnp.sin(angles)[:, None, :]
    first_half = values[..., :half]
    second_half = values[..., half:]
    return jnp.concatenate(
        [first_half * cosine - second_half * sine, second_half * cosine + first_half * sine],
        axis=-1,
    )


def attend_kernel(meta, query_ref, own_ref, received_ref, qp_ref, qw_ref, kp_ref, kw_ref, out_ref):
    r_index = meta[0]
    plane = received_ref.shape[0]
    steps = kp_ref.shape[0]
    heads = query_ref.shape[0]
    scale = 1.0 / query_ref.shape[-1] ** 0.5
    qp = qp_ref[...]
    qw = qw_ref[...]

    def one_step(head, keys, values, back, carry):
        accum, total, top = carry
        scores = lax.dot_general(
            query_ref[head], keys, (((1,), (1,)), ((), ())), preferred_element_type=jnp.float32
        ) * scale
        allowed = (qp == kp_ref[back]) & (kw_ref[back] <= qw)
        scores = jnp.where(allowed, scores, -jnp.inf)
        new_top = jnp.maximum(top, jnp.max(scores, axis=1, keepdims=True))
        fade = jnp.exp(top - new_top)
        weights = jnp.exp(scores - new_top)
        probs = weights.astype(jnp.bfloat16)
        product = jnp.dot(probs, values, preferred_element_type=jnp.float32)
        accum = accum * fade + product
        total = total * fade + jnp.sum(weights, axis=1, keepdims=True)
        return (accum, total, new_top)

    rows, width = query_ref.shape[1], query_ref.shape[2]
    carries = []
    for head in range(heads):
        carry = (
            jnp.zeros((rows, width), jnp.float32),
            jnp.zeros((rows, 1), jnp.float32),
            jnp.full((rows, 1), -jnp.inf, jnp.float32),
        )
        carries.append(one_step(head, own_ref[0, head], own_ref[1, head], 0, carry))

    def body(back, carries):
        source = lax.rem(r_index - back + 2 * plane, plane)
        middle = jnp.logical_and(back > r_index, back <= r_index + plane).astype(jnp.int32)
        return tuple(
            one_step(
                head,
                received_ref[source, middle, 0, head],
                received_ref[source, middle, 1, head],
                back,
                carries[head],
            )
            for head in range(heads)
        )

    carries = lax.fori_loop(1, steps, body, tuple(carries))
    for head in range(heads):
        accum, total, top = carries[head]
        out_ref[head] = (accum / total).astype(out_ref.dtype)


def attend(r_index, query, own_pair, received, q_prompt, q_where, k_prompt, k_where):
    heads, rows, width = query.shape
    steps = k_prompt.shape[0]
    flops = 4 * heads * rows * rows * width * steps
    vmem = pl.BlockSpec(memory_space=pltpu.VMEM)
    return pl.pallas_call(
        attend_kernel,
        out_shape=jax.ShapeDtypeStruct((heads, rows, width), jnp.bfloat16),
        in_specs=[pl.BlockSpec(memory_space=pltpu.SMEM)] + [vmem] * 7,
        out_specs=vmem,
        compiler_params=pltpu.CompilerParams(vmem_limit_bytes=48 * 1024 * 1024),
        cost_estimate=pl.CostEstimate(
            flops=flops,
            transcendentals=heads * rows * rows * steps,
            bytes_accessed=received.size * 2 + own_pair.size * 2 + query.size * 4,
        ),
    )(
        jnp.reshape(r_index, (1,)).astype(jnp.int32),
        query,
        own_pair,
        received,
        q_prompt.reshape(rows, 1).astype(jnp.int32),
        q_where.reshape(rows, 1).astype(jnp.int32),
        k_prompt.reshape(steps, 1, rows).astype(jnp.int32),
        k_where.reshape(steps, 1, rows).astype(jnp.int32),
    )


def on_device(tokens, lengths, w_query, w_key, w_value, w_out, w_gate, w_up, w_down):
    half_type = jnp.bfloat16
    dp = ("y", "r")
    mp = "mp"
    rows = tokens.shape[0]
    narrow = w_query.shape[1]
    shard_rows = w_query.shape[0]
    heads_dev = narrow // HEAD
    dp_index = lax.axis_index(dp)
    mp_index = lax.axis_index(mp)
    mp_size = lax.axis_size(mp)
    y_size = lax.axis_size("y")
    r_size = lax.axis_size("r")
    reach = lax.axis_size(dp) // 2

    down_rows = w_down.shape[0]
    per_mp = down_rows // mp_size
    units_shard = w_gate.shape[1]
    blocks = units_shard // down_rows

    def unit_pieces(w):
        pieces = w.astype(half_type).reshape(shard_rows, blocks, mp_size, per_mp)
        return jnp.transpose(pieces, (2, 0, 1, 3))

    outgoing = [
        unit_pieces(w_gate),
        unit_pieces(w_up),
        w_down.astype(half_type).reshape(mp_size, per_mp, narrow),
        jnp.broadcast_to(w_out.astype(half_type)[None], (mp_size,) + w_out.shape),
    ]
    flat = jnp.concatenate([p.reshape(mp_size, -1) for p in outgoing], axis=1)
    arrived = [flat[mp_index]]
    for step in range(1, mp_size):
        slot = lax.dynamic_index_in_dim(flat, lax.rem(mp_index + step, mp_size), 0, keepdims=False)
        arrived.append(
            lax.ppermute(slot, mp, [(i, (i + step) % mp_size) for i in range(mp_size)])
        )
    got = jnp.stack(arrived)[lax.rem(mp_index - jnp.arange(mp_size) + mp_size, mp_size)]
    kv_shard = jnp.concatenate([w.astype(half_type) for w in (w_key, w_value)], axis=1)
    pieces = []
    at = 0
    for p in outgoing:
        size = p[0].size
        pieces.append(got[:, at : at + size].reshape(p.shape))
        at += size
    gate_got, up_got, down_got, out_got = pieces

    def unit_columns(got_w):
        return jnp.transpose(got_w, (1, 0, 2, 3)).reshape(shard_rows, mp_size * blocks * per_mp)

    gate_shard = unit_columns(gate_got)
    up_shard = unit_columns(up_got)
    down_shard = jnp.transpose(down_got, (1, 0, 2)).reshape(per_mp, mp_size * narrow)
    units = gate_shard.shape[1]
    rest_shard = jnp.concatenate(
        [w_query.astype(half_type), gate_shard, up_shard, down_shard.reshape(shard_rows, -1)], axis=1
    )

    out_full_rows = jnp.transpose(out_got, (1, 0, 2)).reshape(shard_rows, mp_size * narrow)
    swap = [(a * mp_size + b, b * mp_size + a) for a in range(y_size) for b in range(mp_size)]
    out_swapped = lax.ppermute(out_full_rows, ("y", mp), swap)
    server_out = gather_by_exchange(out_swapped, "r")

    kv_full = gather_by_exchange(kv_shard, dp)
    rest_full = lax.all_gather(rest_shard, dp, axis=0, tiled=True)

    normed = layer_norm(tokens).astype(half_type)
    joined_kv = jnp.dot(normed, kv_full, preferred_element_type=jnp.float32)
    q_prompt, q_offset, q_where = prompt_coords(dp_index * rows, rows, lengths)
    shaped = joined_kv.reshape(rows, 2, heads_dev, HEAD)
    keys = rotate(shaped[:, 0], q_offset).astype(half_type)
    values = shaped[:, 1].astype(half_type)
    own_pair = jnp.transpose(jnp.stack((keys, values)), (0, 2, 1, 3))
    plane = r_size
    back_one = shifted(own_pair, dp, plane)
    back_two = shifted(own_pair, dp, 2 * plane)
    own_first = dp_index * rows

    r_index = lax.axis_index("r")
    later = r_index < jnp.arange(plane)
    first_slot = (jnp.arange(2) == 0)[None, :]
    pick_own = (later[:, None] & first_slot)[:, :, None, None, None, None]
    pick_two = (jnp.logical_not(later)[:, None] & first_slot)[:, :, None, None, None, None]
    payload = jnp.where(
        pick_own, own_pair[None, None], jnp.where(pick_two, back_two[None, None], back_one[None, None])
    )
    received = lax.all_to_all(payload, "r", 0, 0, tiled=True)
    received, rest_full = lax.optimization_barrier((received, rest_full))
    q_full = rest_full[:, :narrow]
    server_gate = rest_full[:, narrow : narrow + units]
    server_up = rest_full[:, narrow + units : narrow + 2 * units]
    server_down = rest_full[:, narrow + 2 * units :].reshape(units, -1)
    joined_q = jnp.dot(normed, q_full, preferred_element_type=jnp.float32)
    query = rotate(joined_q.reshape(rows, heads_dev, HEAD), q_offset).astype(half_type)
    query = jnp.transpose(query, (1, 0, 2))
    firsts = own_first - rows * jnp.arange(reach + 1)
    k_prompt, k_offset, k_where = jax.vmap(lambda first: prompt_coords(first, rows, lengths))(firsts)
    context = attend(r_index, query, own_pair, received, q_prompt, q_where, k_prompt, k_where)
    context = jnp.transpose(context, (1, 0, 2)).reshape(rows, narrow)

    partial_out = jnp.dot(context, server_out, preferred_element_type=jnp.float32)
    attended = scatter_sum(partial_out.astype(half_type), mp)
    slab = rows // mp_size
    own_tokens = lax.dynamic_slice_in_dim(tokens, mp_index * slab, slab, 0)
    mixed = (own_tokens.astype(jnp.float32) + attended).astype(half_type)
    normed_own = layer_norm(mixed).astype(half_type)
    normed_two = gather_by_exchange(normed_own, mp)

    gate = jnp.dot(normed_two, server_gate, preferred_element_type=jnp.float32)
    upper = jnp.dot(normed_two, server_up, preferred_element_type=jnp.float32)
    hidden = (jax.nn.silu(gate) * upper).astype(half_type)
    partial_down = jnp.dot(hidden, server_down, preferred_element_type=jnp.float32)
    share = scatter_sum(partial_down.astype(half_type), mp)
    return (mixed.astype(jnp.float32) + share).astype(half_type)


def solution(mesh):
    dp_size, mp_size = mesh.devices.shape
    y_size = mesh.devices.shape[0] // 8 if dp_size % 8 == 0 else 1
    fine = Mesh(mesh.devices.reshape(y_size, dp_size // y_size, mp_size), ("y", "r", "mp"))
    dp = ("y", "r")
    in_specs = (
        P(dp, None),
        P(),
        P(dp, "mp"),
        P(dp, "mp"),
        P(dp, "mp"),
        P(dp, "mp"),
        P(dp, "mp"),
        P(dp, "mp"),
        P(dp, "mp"),
    )
    out_specs = P(("y", "r", "mp"), None)
    return jax.shard_map(
        on_device, mesh=fine, in_specs=in_specs, out_specs=out_specs, check_vma=False
    )
```

```python
import jax
import jax.numpy as jnp
from jax import lax
from jax.sharding import Mesh, PartitionSpec as P
from jax.experimental import pallas as pl
from jax.experimental.pallas import tpu as pltpu

HEAD = 128


epsilon = 1e-05
theta_base = 10000.0


def shifted(value, axis, steps):
    count = lax.axis_size(axis)
    return lax.ppermute(value, axis, [(source, source + steps) for source in range(count - steps)])


def gather_by_exchange(value, axis):
    count = lax.axis_size(axis)
    copies = jnp.broadcast_to(value[None], (count,) + value.shape)
    got = lax.all_to_all(copies, axis, 0, 0, tiled=True)
    return got.reshape((count * value.shape[0],) + value.shape[1:])


def scatter_sum(value, axis):
    count = lax.axis_size(axis)
    pieces = value.reshape((count, value.shape[0] // count) + value.shape[1:])
    got = lax.all_to_all(pieces, axis, 0, 0, tiled=True)
    return jnp.sum(got.astype(jnp.float32), axis=0)


def layer_norm(rows):
    values = rows.astype(jnp.float32)
    centre = jnp.mean(values, axis=-1, keepdims=True)
    spread = jnp.mean(jnp.square(values - centre), axis=-1, keepdims=True)
    return (values - centre) * lax.rsqrt(spread + epsilon)


def prompt_coords(first, count, lengths):
    where = first + jnp.arange(count)
    ends = jnp.cumsum(lengths)
    passed = (ends[None, :] <= where[:, None]).astype(jnp.int32)
    prompt = jnp.sum(passed, axis=1)
    offset = where - jnp.sum(passed * lengths[None, :], axis=1)
    prompt = jnp.where(where < 0, -1, prompt)
    return (prompt, offset, where)


def rotate(values, offset):
    half = values.shape[-1] // 2
    freqs = jnp.power(theta_base, -jnp.arange(half, dtype=jnp.float32) * 2.0 / values.shape[-1])
    angles = offset.astype(jnp.float32)[:, None] * freqs[None, :]
    cosine = jnp.cos(angles)[:, None, :]
    sine = jnp.sin(angles)[:, None, :]
    first_half = values[..., :half]
    second_half = values[..., half:]
    return jnp.concatenate(
        [first_half * cosine - second_half * sine, second_half * cosine + first_half * sine],
        axis=-1,
    )


def attend_kernel(meta, query_ref, own_ref, received_ref, qp_ref, qw_ref, kp_ref, kw_ref, out_ref):
    r_index = meta[0]
    plane = received_ref.shape[0]
    steps = kp_ref.shape[0]
    heads = query_ref.shape[0]
    scale = 1.0 / query_ref.shape[-1] ** 0.5
    qp = qp_ref[...]
    qw = qw_ref[...]

    def one_step(head, keys, values, back, carry):
        accum, total, top = carry
        scores = lax.dot_general(
            query_ref[head], keys, (((1,), (1,)), ((), ())), preferred_element_type=jnp.float32
        ) * scale
        allowed = (qp == kp_ref[back]) & (kw_ref[back] <= qw)
        scores = jnp.where(allowed, scores, -jnp.inf)
        new_top = jnp.maximum(top, jnp.max(scores, axis=1, keepdims=True))
        fade = jnp.exp(top - new_top)
        weights = jnp.exp(scores - new_top)
        probs = weights.astype(jnp.bfloat16)
        product = jnp.dot(probs, values, preferred_element_type=jnp.float32)
        accum = accum * fade + product
        total = total * fade + jnp.sum(weights, axis=1, keepdims=True)
        return (accum, total, new_top)

    rows, width = query_ref.shape[1], query_ref.shape[2]
    carries = []
    for head in range(heads):
        carry = (
            jnp.zeros((rows, width), jnp.float32),
            jnp.zeros((rows, 1), jnp.float32),
            jnp.full((rows, 1), -jnp.inf, jnp.float32),
        )
        carries.append(one_step(head, own_ref[0, head], own_ref[1, head], 0, carry))

    def body(back, carries):
        source = lax.rem(r_index - back + 2 * plane, plane)
        middle = jnp.logical_and(back > r_index, back <= r_index + plane).astype(jnp.int32)
        return tuple(
            one_step(
                head,
                received_ref[source, middle, 0, head],
                received_ref[source, middle, 1, head],
                back,
                carries[head],
            )
            for head in range(heads)
        )

    carries = lax.fori_loop(1, steps, body, tuple(carries))
    for head in range(heads):
        accum, total, top = carries[head]
        out_ref[head] = (accum / total).astype(out_ref.dtype)


def attend(r_index, query, own_pair, received, q_prompt, q_where, k_prompt, k_where):
    heads, rows, width = query.shape
    steps = k_prompt.shape[0]
    flops = 4 * heads * rows * rows * width * steps
    vmem = pl.BlockSpec(memory_space=pltpu.VMEM)
    return pl.pallas_call(
        attend_kernel,
        out_shape=jax.ShapeDtypeStruct((heads, rows, width), jnp.bfloat16),
        in_specs=[pl.BlockSpec(memory_space=pltpu.SMEM)] + [vmem] * 7,
        out_specs=vmem,
        compiler_params=pltpu.CompilerParams(vmem_limit_bytes=48 * 1024 * 1024),
        cost_estimate=pl.CostEstimate(
            flops=flops,
            transcendentals=heads * rows * rows * steps,
            bytes_accessed=received.size * 2 + own_pair.size * 2 + query.size * 4,
        ),
    )(
        jnp.reshape(r_index, (1,)).astype(jnp.int32),
        query,
        own_pair,
        received,
        q_prompt.reshape(rows, 1).astype(jnp.int32),
        q_where.reshape(rows, 1).astype(jnp.int32),
        k_prompt.reshape(steps, 1, rows).astype(jnp.int32),
        k_where.reshape(steps, 1, rows).astype(jnp.int32),
    )


def on_device(tokens, lengths, w_query, w_key, w_value, w_out, w_gate, w_up, w_down):
    half_type = jnp.bfloat16
    dp = ("y", "r")
    mp = "mp"
    rows = tokens.shape[0]
    narrow = w_query.shape[1]
    shard_rows = w_query.shape[0]
    heads_dev = narrow // HEAD
    dp_index = lax.axis_index(dp)
    mp_index = lax.axis_index(mp)
    mp_size = lax.axis_size(mp)
    y_size = lax.axis_size("y")
    r_size = lax.axis_size("r")
    reach = lax.axis_size(dp) // 2

    down_rows = w_down.shape[0]
    per_mp = down_rows // mp_size
    units_shard = w_gate.shape[1]
    blocks = units_shard // down_rows

    def unit_pieces(w):
        pieces = w.astype(half_type).reshape(shard_rows, blocks, mp_size, per_mp)
        return jnp.transpose(pieces, (2, 0, 1, 3))

    outgoing = [
        unit_pieces(w_gate),
        unit_pieces(w_up),
        w_down.astype(half_type).reshape(mp_size, per_mp, narrow),
        jnp.broadcast_to(w_out.astype(half_type)[None], (mp_size,) + w_out.shape),
    ]
    flat = jnp.concatenate([p.reshape(mp_size, -1) for p in outgoing], axis=1)
    got = lax.all_to_all(flat, mp, 0, 0, tiled=True)
    kv_shard = jnp.concatenate([w.astype(half_type) for w in (w_key, w_value)], axis=1)
    got, kv_shard = lax.optimization_barrier((got, kv_shard))
    pieces = []
    at = 0
    for p in outgoing:
        size = p[0].size
        pieces.append(got[:, at : at + size].reshape(p.shape))
        at += size
    gate_got, up_got, down_got, out_got = pieces

    def unit_columns(got_w):
        return jnp.transpose(got_w, (1, 0, 2, 3)).reshape(shard_rows, mp_size * blocks * per_mp)

    gate_shard = unit_columns(gate_got)
    up_shard = unit_columns(up_got)
    down_shard = jnp.transpose(down_got, (1, 0, 2)).reshape(per_mp, mp_size * narrow)
    units = gate_shard.shape[1]
    rest_shard = jnp.concatenate([w_query.astype(half_type), gate_shard, up_shard], axis=1)
    down_part = down_shard.reshape(shard_rows, -1)

    out_full_rows = jnp.transpose(out_got, (1, 0, 2)).reshape(shard_rows, mp_size * narrow)
    swap = [(a * mp_size + b, b * mp_size + a) for a in range(y_size) for b in range(mp_size)]
    out_swapped = lax.ppermute(out_full_rows, ("y", mp), swap)
    server_out = gather_by_exchange(out_swapped, "r")

    kv_full = gather_by_exchange(kv_shard, dp)
    rest_full = lax.all_gather(rest_shard, dp, axis=0, tiled=True)
    down_full = lax.all_gather(down_part, dp, axis=0, tiled=True)

    normed = layer_norm(tokens).astype(half_type)
    joined_kv = jnp.dot(normed, kv_full, preferred_element_type=jnp.float32)
    q_prompt, q_offset, q_where = prompt_coords(dp_index * rows, rows, lengths)
    shaped = joined_kv.reshape(rows, 2, heads_dev, HEAD)
    keys = rotate(shaped[:, 0], q_offset).astype(half_type)
    values = shaped[:, 1].astype(half_type)
    own_pair = jnp.transpose(jnp.stack((keys, values)), (0, 2, 1, 3))
    plane = r_size
    back_one = shifted(own_pair, dp, plane)
    back_two = shifted(own_pair, dp, 2 * plane)
    own_first = dp_index * rows

    r_index = lax.axis_index("r")
    later = r_index < jnp.arange(plane)
    first_slot = (jnp.arange(2) == 0)[None, :]
    pick_own = (later[:, None] & first_slot)[:, :, None, None, None, None]
    pick_two = (jnp.logical_not(later)[:, None] & first_slot)[:, :, None, None, None, None]
    payload = jnp.where(
        pick_own, own_pair[None, None], jnp.where(pick_two, back_two[None, None], back_one[None, None])
    )
    received = lax.all_to_all(payload, "r", 0, 0, tiled=True)
    received, rest_full = lax.optimization_barrier((received, rest_full))
    q_full = rest_full[:, :narrow]
    server_gate = rest_full[:, narrow : narrow + units]
    server_up = rest_full[:, narrow + units : narrow + 2 * units]
    server_down = down_full.reshape(units, -1)
    joined_q = jnp.dot(normed, q_full, preferred_element_type=jnp.float32)
    query = rotate(joined_q.reshape(rows, heads_dev, HEAD), q_offset).astype(half_type)
    query = jnp.transpose(query, (1, 0, 2))
    firsts = own_first - rows * jnp.arange(reach + 1)
    k_prompt, k_offset, k_where = jax.vmap(lambda first: prompt_coords(first, rows, lengths))(firsts)
    context = attend(r_index, query, own_pair, received, q_prompt, q_where, k_prompt, k_where)
    context = jnp.transpose(context, (1, 0, 2)).reshape(rows, narrow)

    partial_out = jnp.dot(context, server_out, preferred_element_type=jnp.float32)
    attended = scatter_sum(partial_out.astype(half_type), mp)
    slab = rows // mp_size
    own_tokens = lax.dynamic_slice_in_dim(tokens, mp_index * slab, slab, 0)
    mixed = (own_tokens.astype(jnp.float32) + attended).astype(half_type)
    normed_own = layer_norm(mixed).astype(half_type)
    normed_two = gather_by_exchange(normed_own, mp)

    gate = jnp.dot(normed_two, server_gate, preferred_element_type=jnp.float32)
    upper = jnp.dot(normed_two, server_up, preferred_element_type=jnp.float32)
    hidden = (jax.nn.silu(gate) * upper).astype(half_type)
    partial_down = jnp.dot(hidden, server_down, preferred_element_type=jnp.float32)
    share = scatter_sum(partial_down.astype(half_type), mp)
    return (mixed.astype(jnp.float32) + share).astype(half_type)


def solution(mesh):
    dp_size, mp_size = mesh.devices.shape
    y_size = mesh.devices.shape[0] // 8 if dp_size % 8 == 0 else 1
    fine = Mesh(mesh.devices.reshape(y_size, dp_size // y_size, mp_size), ("y", "r", "mp"))
    dp = ("y", "r")
    in_specs = (
        P(dp, None),
        P(),
        P(dp, "mp"),
        P(dp, "mp"),
        P(dp, "mp"),
        P(dp, "mp"),
        P(dp, "mp"),
        P(dp, "mp"),
        P(dp, "mp"),
    )
    out_specs = P(("y", "r", "mp"), None)
    return jax.shard_map(
        on_device, mesh=fine, in_specs=in_specs, out_specs=out_specs, check_vma=False
    )
```

```python
import jax
import jax.numpy as jnp
from jax import lax
from jax.sharding import Mesh, PartitionSpec as P
from jax.experimental import pallas as pl
from jax.experimental.pallas import tpu as pltpu

HEAD = 128


epsilon = 1e-05
theta_base = 10000.0


def shifted(value, axis, steps):
    count = lax.axis_size(axis)
    return lax.ppermute(value, axis, [(source, source + steps) for source in range(count - steps)])


def gather_by_exchange(value, axis):
    count = lax.axis_size(axis)
    copies = jnp.broadcast_to(value[None], (count,) + value.shape)
    got = lax.all_to_all(copies, axis, 0, 0, tiled=True)
    return got.reshape((count * value.shape[0],) + value.shape[1:])


def scatter_sum(value, axis):
    count = lax.axis_size(axis)
    pieces = value.reshape((count, value.shape[0] // count) + value.shape[1:])
    got = lax.all_to_all(pieces, axis, 0, 0, tiled=True)
    return jnp.sum(got.astype(jnp.float32), axis=0)


def layer_norm(rows):
    values = rows.astype(jnp.float32)
    centre = jnp.mean(values, axis=-1, keepdims=True)
    spread = jnp.mean(jnp.square(values - centre), axis=-1, keepdims=True)
    return (values - centre) * lax.rsqrt(spread + epsilon)


def prompt_coords(first, count, lengths):
    where = first + jnp.arange(count)
    ends = jnp.cumsum(lengths)
    passed = (ends[None, :] <= where[:, None]).astype(jnp.int32)
    prompt = jnp.sum(passed, axis=1)
    offset = where - jnp.sum(passed * lengths[None, :], axis=1)
    prompt = jnp.where(where < 0, -1, prompt)
    return (prompt, offset, where)


def rotate(values, offset):
    half = values.shape[-1] // 2
    freqs = jnp.power(theta_base, -jnp.arange(half, dtype=jnp.float32) * 2.0 / values.shape[-1])
    angles = offset.astype(jnp.float32)[:, None] * freqs[None, :]
    cosine = jnp.cos(angles)[:, None, :]
    sine = jnp.sin(angles)[:, None, :]
    first_half = values[..., :half]
    second_half = values[..., half:]
    return jnp.concatenate(
        [first_half * cosine - second_half * sine, second_half * cosine + first_half * sine],
        axis=-1,
    )


def attend_kernel(meta, query_ref, own_ref, received_ref, qp_ref, qw_ref, kp_ref, kw_ref, out_ref):
    r_index = meta[0]
    plane = received_ref.shape[0]
    steps = kp_ref.shape[0]
    heads = query_ref.shape[0]
    scale = 1.0 / query_ref.shape[-1] ** 0.5
    qp = qp_ref[...]
    qw = qw_ref[...]

    def one_step(head, keys, values, back, carry):
        accum, total, top = carry
        scores = lax.dot_general(
            query_ref[head], keys, (((1,), (1,)), ((), ())), preferred_element_type=jnp.float32
        ) * scale
        allowed = (qp == kp_ref[back]) & (kw_ref[back] <= qw)
        scores = jnp.where(allowed, scores, -jnp.inf)
        new_top = jnp.maximum(top, jnp.max(scores, axis=1, keepdims=True))
        fade = jnp.exp(top - new_top)
        weights = jnp.exp(scores - new_top)
        probs = weights.astype(jnp.bfloat16)
        product = jnp.dot(probs, values, preferred_element_type=jnp.float32)
        accum = accum * fade + product
        total = total * fade + jnp.sum(weights, axis=1, keepdims=True)
        return (accum, total, new_top)

    rows, width = query_ref.shape[1], query_ref.shape[2]
    carries = []
    for head in range(heads):
        carry = (
            jnp.zeros((rows, width), jnp.float32),
            jnp.zeros((rows, 1), jnp.float32),
            jnp.full((rows, 1), -jnp.inf, jnp.float32),
        )
        carries.append(one_step(head, own_ref[0, head], own_ref[1, head], 0, carry))

    def body(back, carries):
        source = lax.rem(r_index - back + 2 * plane, plane)
        middle = jnp.logical_and(back > r_index, back <= r_index + plane).astype(jnp.int32)
        return tuple(
            one_step(
                head,
                received_ref[source, middle, 0, head],
                received_ref[source, middle, 1, head],
                back,
                carries[head],
            )
            for head in range(heads)
        )

    carries = lax.fori_loop(1, steps, body, tuple(carries))
    for head in range(heads):
        accum, total, top = carries[head]
        out_ref[head] = (accum / total).astype(out_ref.dtype)


def attend(r_index, query, own_pair, received, q_prompt, q_where, k_prompt, k_where):
    heads, rows, width = query.shape
    steps = k_prompt.shape[0]
    flops = 4 * heads * rows * rows * width * steps
    vmem = pl.BlockSpec(memory_space=pltpu.VMEM)
    return pl.pallas_call(
        attend_kernel,
        out_shape=jax.ShapeDtypeStruct((heads, rows, width), jnp.bfloat16),
        in_specs=[pl.BlockSpec(memory_space=pltpu.SMEM)] + [vmem] * 7,
        out_specs=vmem,
        compiler_params=pltpu.CompilerParams(vmem_limit_bytes=48 * 1024 * 1024),
        cost_estimate=pl.CostEstimate(
            flops=flops,
            transcendentals=heads * rows * rows * steps,
            bytes_accessed=received.size * 2 + own_pair.size * 2 + query.size * 4,
        ),
    )(
        jnp.reshape(r_index, (1,)).astype(jnp.int32),
        query,
        own_pair,
        received,
        q_prompt.reshape(rows, 1).astype(jnp.int32),
        q_where.reshape(rows, 1).astype(jnp.int32),
        k_prompt.reshape(steps, 1, rows).astype(jnp.int32),
        k_where.reshape(steps, 1, rows).astype(jnp.int32),
    )


def on_device(tokens, lengths, w_query, w_key, w_value, w_out, w_gate, w_up, w_down):
    half_type = jnp.bfloat16
    dp = ("y", "r")
    mp = "mp"
    rows = tokens.shape[0]
    narrow = w_query.shape[1]
    shard_rows = w_query.shape[0]
    heads_dev = narrow // HEAD
    dp_index = lax.axis_index(dp)
    mp_index = lax.axis_index(mp)
    mp_size = lax.axis_size(mp)
    y_size = lax.axis_size("y")
    r_size = lax.axis_size("r")
    reach = lax.axis_size(dp) // 2

    down_rows = w_down.shape[0]
    per_mp = down_rows // mp_size
    units_shard = w_gate.shape[1]
    blocks = units_shard // down_rows

    def unit_pieces(w):
        pieces = w.astype(half_type).reshape(shard_rows, blocks, mp_size, per_mp)
        return jnp.transpose(pieces, (2, 0, 1, 3))

    outgoing = [
        unit_pieces(w_gate),
        unit_pieces(w_up),
        w_down.astype(half_type).reshape(mp_size, per_mp, narrow),
        jnp.broadcast_to(w_out.astype(half_type)[None], (mp_size,) + w_out.shape),
    ]
    flat = jnp.concatenate([p.reshape(mp_size, -1) for p in outgoing], axis=1)
    got = lax.all_to_all(flat, mp, 0, 0, tiled=True)
    kv_shard = jnp.concatenate([w.astype(half_type) for w in (w_key, w_value)], axis=1)
    got, kv_shard = lax.optimization_barrier((got, kv_shard))
    pieces = []
    at = 0
    for p in outgoing:
        size = p[0].size
        pieces.append(got[:, at : at + size].reshape(p.shape))
        at += size
    gate_got, up_got, down_got, out_got = pieces

    def unit_columns(got_w):
        return jnp.transpose(got_w, (1, 0, 2, 3)).reshape(shard_rows, mp_size * blocks * per_mp)

    gate_shard = unit_columns(gate_got)
    up_shard = unit_columns(up_got)
    down_shard = jnp.transpose(down_got, (1, 0, 2)).reshape(per_mp, mp_size * narrow)
    units = gate_shard.shape[1]
    rest_shard = jnp.concatenate([w_query.astype(half_type), gate_shard, up_shard], axis=1)

    out_full_rows = jnp.transpose(out_got, (1, 0, 2)).reshape(shard_rows, mp_size * narrow)
    swap = [(a * mp_size + b, b * mp_size + a) for a in range(y_size) for b in range(mp_size)]
    out_swapped = lax.ppermute(out_full_rows, ("y", mp), swap)
    server_out = gather_by_exchange(out_swapped, "r")

    kv_full = gather_by_exchange(kv_shard, dp)
    rest_full = lax.all_gather(rest_shard, dp, axis=0, tiled=True)
    down_full = lax.all_gather(down_shard, dp, axis=0, tiled=True)

    normed = layer_norm(tokens).astype(half_type)
    joined_kv = jnp.dot(normed, kv_full, preferred_element_type=jnp.float32)
    q_prompt, q_offset, q_where = prompt_coords(dp_index * rows, rows, lengths)
    shaped = joined_kv.reshape(rows, 2, heads_dev, HEAD)
    keys = rotate(shaped[:, 0], q_offset).astype(half_type)
    values = shaped[:, 1].astype(half_type)
    own_pair = jnp.transpose(jnp.stack((keys, values)), (0, 2, 1, 3))
    plane = r_size
    back_one = shifted(own_pair, dp, plane)
    back_two = shifted(own_pair, dp, 2 * plane)
    own_first = dp_index * rows

    r_index = lax.axis_index("r")
    later = r_index < jnp.arange(plane)
    first_slot = (jnp.arange(2) == 0)[None, :]
    pick_own = (later[:, None] & first_slot)[:, :, None, None, None, None]
    pick_two = (jnp.logical_not(later)[:, None] & first_slot)[:, :, None, None, None, None]
    payload = jnp.where(
        pick_own, own_pair[None, None], jnp.where(pick_two, back_two[None, None], back_one[None, None])
    )
    received = lax.all_to_all(payload, "r", 0, 0, tiled=True)
    received, rest_full = lax.optimization_barrier((received, rest_full))
    q_full = rest_full[:, :narrow]
    server_gate = rest_full[:, narrow : narrow + units]
    server_up = rest_full[:, narrow + units : narrow + 2 * units]
    server_down = down_full
    joined_q = jnp.dot(normed, q_full, preferred_element_type=jnp.float32)
    query = rotate(joined_q.reshape(rows, heads_dev, HEAD), q_offset).astype(half_type)
    query = jnp.transpose(query, (1, 0, 2))
    firsts = own_first - rows * jnp.arange(reach + 1)
    k_prompt, k_offset, k_where = jax.vmap(lambda first: prompt_coords(first, rows, lengths))(firsts)
    context = attend(r_index, query, own_pair, received, q_prompt, q_where, k_prompt, k_where)
    context = jnp.transpose(context, (1, 0, 2)).reshape(rows, narrow)

    partial_out = jnp.dot(context, server_out, preferred_element_type=jnp.float32)
    attended = scatter_sum(partial_out.astype(half_type), mp)
    slab = rows // mp_size
    own_tokens = lax.dynamic_slice_in_dim(tokens, mp_index * slab, slab, 0)
    mixed = (own_tokens.astype(jnp.float32) + attended).astype(half_type)
    normed_own = layer_norm(mixed).astype(half_type)
    normed_two = gather_by_exchange(normed_own, mp)

    gate = jnp.dot(normed_two, server_gate, preferred_element_type=jnp.float32)
    upper = jnp.dot(normed_two, server_up, preferred_element_type=jnp.float32)
    hidden = (jax.nn.silu(gate) * upper).astype(half_type)
    partial_down = jnp.dot(hidden, server_down, preferred_element_type=jnp.float32)
    share = scatter_sum(partial_down.astype(half_type), mp)
    return (mixed.astype(jnp.float32) + share).astype(half_type)


def solution(mesh):
    dp_size, mp_size = mesh.devices.shape
    y_size = mesh.devices.shape[0] // 8 if dp_size % 8 == 0 else 1
    fine = Mesh(mesh.devices.reshape(y_size, dp_size // y_size, mp_size), ("y", "r", "mp"))
    dp = ("y", "r")
    in_specs = (
        P(dp, None),
        P(),
        P(dp, "mp"),
        P(dp, "mp"),
        P(dp, "mp"),
        P(dp, "mp"),
        P(dp, "mp"),
        P(dp, "mp"),
        P(dp, "mp"),
    )
    out_specs = P(("y", "r", "mp"), None)
    return jax.shard_map(
        on_device, mesh=fine, in_specs=in_specs, out_specs=out_specs, check_vma=False
    )
```

```python
import jax
import jax.numpy as jnp
from jax import lax
from jax.sharding import Mesh, PartitionSpec as P
from jax.experimental import pallas as pl
from jax.experimental.pallas import tpu as pltpu

HEAD = 128


epsilon = 1e-05
theta_base = 10000.0


def shifted(value, axis, steps):
    count = lax.axis_size(axis)
    return lax.ppermute(value, axis, [(source, source + steps) for source in range(count - steps)])


def gather_by_exchange(value, axis):
    count = lax.axis_size(axis)
    copies = jnp.broadcast_to(value[None], (count,) + value.shape)
    got = lax.all_to_all(copies, axis, 0, 0, tiled=True)
    return got.reshape((count * value.shape[0],) + value.shape[1:])


def scatter_sum(value, axis):
    count = lax.axis_size(axis)
    pieces = value.reshape((count, value.shape[0] // count) + value.shape[1:])
    got = lax.all_to_all(pieces, axis, 0, 0, tiled=True)
    return jnp.sum(got.astype(jnp.float32), axis=0)


def layer_norm(rows):
    values = rows.astype(jnp.float32)
    centre = jnp.mean(values, axis=-1, keepdims=True)
    spread = jnp.mean(jnp.square(values - centre), axis=-1, keepdims=True)
    return (values - centre) * lax.rsqrt(spread + epsilon)


def prompt_coords(first, count, lengths):
    where = first + jnp.arange(count)
    ends = jnp.cumsum(lengths)
    passed = (ends[None, :] <= where[:, None]).astype(jnp.int32)
    prompt = jnp.sum(passed, axis=1)
    offset = where - jnp.sum(passed * lengths[None, :], axis=1)
    prompt = jnp.where(where < 0, -1, prompt)
    return (prompt, offset, where)


def rotate(values, offset):
    half = values.shape[-1] // 2
    freqs = jnp.power(theta_base, -jnp.arange(half, dtype=jnp.float32) * 2.0 / values.shape[-1])
    angles = offset.astype(jnp.float32)[:, None] * freqs[None, :]
    cosine = jnp.cos(angles)[:, None, :]
    sine = jnp.sin(angles)[:, None, :]
    first_half = values[..., :half]
    second_half = values[..., half:]
    return jnp.concatenate(
        [first_half * cosine - second_half * sine, second_half * cosine + first_half * sine],
        axis=-1,
    )


def attend_kernel(meta, query_ref, own_ref, received_ref, qp_ref, qw_ref, kp_ref, kw_ref, out_ref):
    r_index = meta[0]
    plane = received_ref.shape[0]
    steps = kp_ref.shape[0]
    heads = query_ref.shape[0]
    scale = 1.0 / query_ref.shape[-1] ** 0.5
    qp = qp_ref[...]
    qw = qw_ref[...]

    def one_step(head, keys, values, back, carry):
        accum, total, top = carry
        scores = lax.dot_general(
            query_ref[head], keys, (((1,), (1,)), ((), ())), preferred_element_type=jnp.float32
        ) * scale
        allowed = (qp == kp_ref[back]) & (kw_ref[back] <= qw)
        scores = jnp.where(allowed, scores, -jnp.inf)
        new_top = jnp.maximum(top, jnp.max(scores, axis=1, keepdims=True))
        fade = jnp.exp(top - new_top)
        weights = jnp.exp(scores - new_top)
        probs = weights.astype(jnp.bfloat16)
        product = jnp.dot(probs, values, preferred_element_type=jnp.float32)
        accum = accum * fade + product
        total = total * fade + jnp.sum(weights, axis=1, keepdims=True)
        return (accum, total, new_top)

    rows, width = query_ref.shape[1], query_ref.shape[2]
    carries = []
    for head in range(heads):
        carry = (
            jnp.zeros((rows, width), jnp.float32),
            jnp.zeros((rows, 1), jnp.float32),
            jnp.full((rows, 1), -jnp.inf, jnp.float32),
        )
        carries.append(one_step(head, own_ref[0, head], own_ref[1, head], 0, carry))

    def body(back, carries):
        source = lax.rem(r_index - back + 2 * plane, plane)
        middle = jnp.logical_and(back > r_index, back <= r_index + plane).astype(jnp.int32)
        return tuple(
            one_step(
                head,
                received_ref[source, middle, 0, head],
                received_ref[source, middle, 1, head],
                back,
                carries[head],
            )
            for head in range(heads)
        )

    carries = lax.fori_loop(1, steps, body, tuple(carries))
    for head in range(heads):
        accum, total, top = carries[head]
        out_ref[head] = (accum / total).astype(out_ref.dtype)


def attend(r_index, query, own_pair, received, q_prompt, q_where, k_prompt, k_where):
    heads, rows, width = query.shape
    steps = k_prompt.shape[0]
    flops = 4 * heads * rows * rows * width * steps
    vmem = pl.BlockSpec(memory_space=pltpu.VMEM)
    return pl.pallas_call(
        attend_kernel,
        out_shape=jax.ShapeDtypeStruct((heads, rows, width), jnp.bfloat16),
        in_specs=[pl.BlockSpec(memory_space=pltpu.SMEM)] + [vmem] * 7,
        out_specs=vmem,
        compiler_params=pltpu.CompilerParams(vmem_limit_bytes=48 * 1024 * 1024),
        cost_estimate=pl.CostEstimate(
            flops=flops,
            transcendentals=heads * rows * rows * steps,
            bytes_accessed=received.size * 2 + own_pair.size * 2 + query.size * 4,
        ),
    )(
        jnp.reshape(r_index, (1,)).astype(jnp.int32),
        query,
        own_pair,
        received,
        q_prompt.reshape(rows, 1).astype(jnp.int32),
        q_where.reshape(rows, 1).astype(jnp.int32),
        k_prompt.reshape(steps, 1, rows).astype(jnp.int32),
        k_where.reshape(steps, 1, rows).astype(jnp.int32),
    )


def on_device(tokens, lengths, w_query, w_key, w_value, w_out, w_gate, w_up, w_down):
    half_type = jnp.bfloat16
    dp = ("y", "r")
    mp = "mp"
    rows = tokens.shape[0]
    narrow = w_query.shape[1]
    shard_rows = w_query.shape[0]
    heads_dev = narrow // HEAD
    dp_index = lax.axis_index(dp)
    mp_index = lax.axis_index(mp)
    mp_size = lax.axis_size(mp)
    y_size = lax.axis_size("y")
    r_size = lax.axis_size("r")
    reach = lax.axis_size(dp) // 2

    down_rows = w_down.shape[0]
    per_mp = down_rows // mp_size
    units_shard = w_gate.shape[1]
    blocks = units_shard // down_rows

    def unit_pieces(w):
        pieces = w.astype(half_type).reshape(shard_rows, blocks, mp_size, per_mp)
        return jnp.transpose(pieces, (2, 0, 1, 3))

    outgoing = [
        unit_pieces(w_gate),
        unit_pieces(w_up),
        w_down.astype(half_type).reshape(mp_size, per_mp, narrow),
        jnp.broadcast_to(w_out.astype(half_type)[None], (mp_size,) + w_out.shape),
    ]
    flat = jnp.concatenate([p.reshape(mp_size, -1) for p in outgoing], axis=1)
    got = lax.all_to_all(flat, mp, 0, 0, tiled=True)
    kv_shard = jnp.concatenate([w.astype(half_type) for w in (w_key, w_value)], axis=1)
    got, kv_shard = lax.optimization_barrier((got, kv_shard))
    pieces = []
    at = 0
    for p in outgoing:
        size = p[0].size
        pieces.append(got[:, at : at + size].reshape(p.shape))
        at += size
    gate_got, up_got, down_got, out_got = pieces

    def unit_columns(got_w):
        return jnp.transpose(got_w, (1, 0, 2, 3)).reshape(shard_rows, mp_size * blocks * per_mp)

    gate_shard = unit_columns(gate_got)
    up_shard = unit_columns(up_got)
    down_shard = jnp.transpose(down_got, (1, 0, 2)).reshape(per_mp, mp_size * narrow)
    units = gate_shard.shape[1]
    rest_shard = jnp.concatenate([w_query.astype(half_type), gate_shard], axis=1)
    late_shard = jnp.concatenate([up_shard, down_shard.reshape(shard_rows, -1)], axis=1)

    out_full_rows = jnp.transpose(out_got, (1, 0, 2)).reshape(shard_rows, mp_size * narrow)
    swap = [(a * mp_size + b, b * mp_size + a) for a in range(y_size) for b in range(mp_size)]
    out_swapped = lax.ppermute(out_full_rows, ("y", mp), swap)
    server_out = gather_by_exchange(out_swapped, "r")

    kv_full = gather_by_exchange(kv_shard, dp)
    rest_full = lax.all_gather(rest_shard, dp, axis=0, tiled=True)
    late_full = lax.all_gather(late_shard, dp, axis=0, tiled=True)

    normed = layer_norm(tokens).astype(half_type)
    joined_kv = jnp.dot(normed, kv_full, preferred_element_type=jnp.float32)
    q_prompt, q_offset, q_where = prompt_coords(dp_index * rows, rows, lengths)
    shaped = joined_kv.reshape(rows, 2, heads_dev, HEAD)
    keys = rotate(shaped[:, 0], q_offset).astype(half_type)
    values = shaped[:, 1].astype(half_type)
    own_pair = jnp.transpose(jnp.stack((keys, values)), (0, 2, 1, 3))
    plane = r_size
    back_one = shifted(own_pair, dp, plane)
    back_two = shifted(own_pair, dp, 2 * plane)
    own_first = dp_index * rows

    r_index = lax.axis_index("r")
    later = r_index < jnp.arange(plane)
    first_slot = (jnp.arange(2) == 0)[None, :]
    pick_own = (later[:, None] & first_slot)[:, :, None, None, None, None]
    pick_two = (jnp.logical_not(later)[:, None] & first_slot)[:, :, None, None, None, None]
    payload = jnp.where(
        pick_own, own_pair[None, None], jnp.where(pick_two, back_two[None, None], back_one[None, None])
    )
    received = lax.all_to_all(payload, "r", 0, 0, tiled=True)
    received, rest_full = lax.optimization_barrier((received, rest_full))
    q_full = rest_full[:, :narrow]
    server_gate = rest_full[:, narrow : narrow + units]
    server_up = late_full[:, :units]
    server_down = late_full[:, units:].reshape(units, -1)
    joined_q = jnp.dot(normed, q_full, preferred_element_type=jnp.float32)
    query = rotate(joined_q.reshape(rows, heads_dev, HEAD), q_offset).astype(half_type)
    query = jnp.transpose(query, (1, 0, 2))
    firsts = own_first - rows * jnp.arange(reach + 1)
    k_prompt, k_offset, k_where = jax.vmap(lambda first: prompt_coords(first, rows, lengths))(firsts)
    context = attend(r_index, query, own_pair, received, q_prompt, q_where, k_prompt, k_where)
    context = jnp.transpose(context, (1, 0, 2)).reshape(rows, narrow)

    partial_out = jnp.dot(context, server_out, preferred_element_type=jnp.float32)
    attended = scatter_sum(partial_out.astype(half_type), mp)
    slab = rows // mp_size
    own_tokens = lax.dynamic_slice_in_dim(tokens, mp_index * slab, slab, 0)
    mixed = (own_tokens.astype(jnp.float32) + attended).astype(half_type)
    normed_own = layer_norm(mixed).astype(half_type)
    normed_two = gather_by_exchange(normed_own, mp)

    gate = jnp.dot(normed_two, server_gate, preferred_element_type=jnp.float32)
    upper = jnp.dot(normed_two, server_up, preferred_element_type=jnp.float32)
    hidden = (jax.nn.silu(gate) * upper).astype(half_type)
    partial_down = jnp.dot(hidden, server_down, preferred_element_type=jnp.float32)
    share = scatter_sum(partial_down.astype(half_type), mp)
    return (mixed.astype(jnp.float32) + share).astype(half_type)


def solution(mesh):
    dp_size, mp_size = mesh.devices.shape
    y_size = mesh.devices.shape[0] // 8 if dp_size % 8 == 0 else 1
    fine = Mesh(mesh.devices.reshape(y_size, dp_size // y_size, mp_size), ("y", "r", "mp"))
    dp = ("y", "r")
    in_specs = (
        P(dp, None),
        P(),
        P(dp, "mp"),
        P(dp, "mp"),
        P(dp, "mp"),
        P(dp, "mp"),
        P(dp, "mp"),
        P(dp, "mp"),
        P(dp, "mp"),
    )
    out_specs = P(("y", "r", "mp"), None)
    return jax.shard_map(
        on_device, mesh=fine, in_specs=in_specs, out_specs=out_specs, check_vma=False
    )
```

```python
import jax
import jax.numpy as jnp
from jax import lax
from jax.sharding import Mesh, PartitionSpec as P
from jax.experimental import pallas as pl
from jax.experimental.pallas import tpu as pltpu

HEAD = 128


epsilon = 1e-05
theta_base = 10000.0


def shifted(value, axis, steps):
    count = lax.axis_size(axis)
    return lax.ppermute(value, axis, [(source, source + steps) for source in range(count - steps)])


def gather_by_exchange(value, axis):
    count = lax.axis_size(axis)
    copies = jnp.broadcast_to(value[None], (count,) + value.shape)
    got = lax.all_to_all(copies, axis, 0, 0, tiled=True)
    return got.reshape((count * value.shape[0],) + value.shape[1:])


def scatter_sum(value, axis):
    count = lax.axis_size(axis)
    pieces = value.reshape((count, value.shape[0] // count) + value.shape[1:])
    got = lax.all_to_all(pieces, axis, 0, 0, tiled=True)
    return jnp.sum(got.astype(jnp.float32), axis=0)


def layer_norm(rows):
    values = rows.astype(jnp.float32)
    centre = jnp.mean(values, axis=-1, keepdims=True)
    spread = jnp.mean(jnp.square(values - centre), axis=-1, keepdims=True)
    return (values - centre) * lax.rsqrt(spread + epsilon)


def prompt_coords(first, count, lengths):
    where = first + jnp.arange(count)
    ends = jnp.cumsum(lengths)
    passed = (ends[None, :] <= where[:, None]).astype(jnp.int32)
    prompt = jnp.sum(passed, axis=1)
    offset = where - jnp.sum(passed * lengths[None, :], axis=1)
    prompt = jnp.where(where < 0, -1, prompt)
    return (prompt, offset, where)


def rotate(values, offset):
    half = values.shape[-1] // 2
    freqs = jnp.power(theta_base, -jnp.arange(half, dtype=jnp.float32) * 2.0 / values.shape[-1])
    angles = offset.astype(jnp.float32)[:, None] * freqs[None, :]
    cosine = jnp.cos(angles)[:, None, :]
    sine = jnp.sin(angles)[:, None, :]
    first_half = values[..., :half]
    second_half = values[..., half:]
    return jnp.concatenate(
        [first_half * cosine - second_half * sine, second_half * cosine + first_half * sine],
        axis=-1,
    )


def attend_kernel(meta, query_ref, own_ref, received_ref, qp_ref, qw_ref, kp_ref, kw_ref, out_ref):
    r_index = meta[0]
    plane = received_ref.shape[0]
    steps = kp_ref.shape[0]
    heads = query_ref.shape[0]
    scale = 1.0 / query_ref.shape[-1] ** 0.5
    qp = qp_ref[...]
    qw = qw_ref[...]

    def one_step(head, keys, values, back, carry):
        accum, total, top = carry
        scores = lax.dot_general(
            query_ref[head], keys, (((1,), (1,)), ((), ())), preferred_element_type=jnp.float32
        ) * scale
        allowed = (qp == kp_ref[back]) & (kw_ref[back] <= qw)
        scores = jnp.where(allowed, scores, -jnp.inf)
        new_top = jnp.maximum(top, jnp.max(scores, axis=1, keepdims=True))
        fade = jnp.exp(top - new_top)
        weights = jnp.exp(scores - new_top)
        probs = weights.astype(jnp.bfloat16)
        product = jnp.dot(probs, values, preferred_element_type=jnp.float32)
        accum = accum * fade + product
        total = total * fade + jnp.sum(weights, axis=1, keepdims=True)
        return (accum, total, new_top)

    rows, width = query_ref.shape[1], query_ref.shape[2]
    carries = []
    for head in range(heads):
        carry = (
            jnp.zeros((rows, width), jnp.float32),
            jnp.zeros((rows, 1), jnp.float32),
            jnp.full((rows, 1), -jnp.inf, jnp.float32),
        )
        carries.append(one_step(head, own_ref[0, head], own_ref[1, head], 0, carry))

    def body(back, carries):
        source = lax.rem(r_index - back + 2 * plane, plane)
        middle = jnp.logical_and(back > r_index, back <= r_index + plane).astype(jnp.int32)
        return tuple(
            one_step(
                head,
                received_ref[source, middle, 0, head],
                received_ref[source, middle, 1, head],
                back,
                carries[head],
            )
            for head in range(heads)
        )

    carries = lax.fori_loop(1, steps, body, tuple(carries))
    for head in range(heads):
        accum, total, top = carries[head]
        out_ref[head] = (accum / total).astype(out_ref.dtype)


def attend(r_index, query, own_pair, received, q_prompt, q_where, k_prompt, k_where):
    heads, rows, width = query.shape
    steps = k_prompt.shape[0]
    flops = 4 * heads * rows * rows * width * steps
    vmem = pl.BlockSpec(memory_space=pltpu.VMEM)
    return pl.pallas_call(
        attend_kernel,
        out_shape=jax.ShapeDtypeStruct((heads, rows, width), jnp.bfloat16),
        in_specs=[pl.BlockSpec(memory_space=pltpu.SMEM)] + [vmem] * 7,
        out_specs=vmem,
        compiler_params=pltpu.CompilerParams(vmem_limit_bytes=48 * 1024 * 1024),
        cost_estimate=pl.CostEstimate(
            flops=flops,
            transcendentals=heads * rows * rows * steps,
            bytes_accessed=received.size * 2 + own_pair.size * 2 + query.size * 4,
        ),
    )(
        jnp.reshape(r_index, (1,)).astype(jnp.int32),
        query,
        own_pair,
        received,
        q_prompt.reshape(rows, 1).astype(jnp.int32),
        q_where.reshape(rows, 1).astype(jnp.int32),
        k_prompt.reshape(steps, 1, rows).astype(jnp.int32),
        k_where.reshape(steps, 1, rows).astype(jnp.int32),
    )


def on_device(tokens, lengths, w_query, w_key, w_value, w_out, w_gate, w_up, w_down):
    half_type = jnp.bfloat16
    dp = ("y", "r")
    mp = "mp"
    rows = tokens.shape[0]
    narrow = w_query.shape[1]
    shard_rows = w_query.shape[0]
    heads_dev = narrow // HEAD
    dp_index = lax.axis_index(dp)
    mp_index = lax.axis_index(mp)
    mp_size = lax.axis_size(mp)
    y_size = lax.axis_size("y")
    r_size = lax.axis_size("r")
    reach = lax.axis_size(dp) // 2

    down_rows = w_down.shape[0]
    per_mp = down_rows // mp_size
    units_shard = w_gate.shape[1]
    blocks = units_shard // down_rows

    def unit_pieces(w):
        pieces = w.astype(half_type).reshape(shard_rows, blocks, mp_size, per_mp)
        return jnp.transpose(pieces, (2, 0, 1, 3))

    outgoing = [
        unit_pieces(w_gate),
        unit_pieces(w_up),
        w_down.astype(half_type).reshape(mp_size, per_mp, narrow),
        jnp.broadcast_to(w_out.astype(half_type)[None], (mp_size,) + w_out.shape),
    ]
    flat = jnp.concatenate([p.reshape(mp_size, -1) for p in outgoing], axis=1)
    got = lax.all_to_all(flat, mp, 0, 0, tiled=True)
    kv_shard = jnp.concatenate([w.astype(half_type) for w in (w_key, w_value)], axis=1)
    got, kv_shard = lax.optimization_barrier((got, kv_shard))
    pieces = []
    at = 0
    for p in outgoing:
        size = p[0].size
        pieces.append(got[:, at : at + size].reshape(p.shape))
        at += size
    gate_got, up_got, down_got, out_got = pieces

    def unit_columns(got_w):
        return jnp.transpose(got_w, (1, 0, 2, 3)).reshape(shard_rows, mp_size * blocks * per_mp)

    gate_shard = unit_columns(gate_got)
    up_shard = unit_columns(up_got)
    down_shard = jnp.transpose(down_got, (1, 0, 2)).reshape(per_mp, mp_size * narrow)
    units = gate_shard.shape[1]
    rest_shard = jnp.concatenate([w_query.astype(half_type), gate_shard, up_shard], axis=1)

    out_full_rows = jnp.transpose(out_got, (1, 0, 2)).reshape(shard_rows, mp_size * narrow)
    swap = [(a * mp_size + b, b * mp_size + a) for a in range(y_size) for b in range(mp_size)]
    out_swapped = lax.ppermute(out_full_rows, ("y", mp), swap)
    server_out = gather_by_exchange(out_swapped, "r")

    kv_full = gather_by_exchange(kv_shard, dp)
    rest_full = lax.all_gather(rest_shard, dp, axis=0, tiled=True)
    down_full = lax.all_gather(down_shard, dp, axis=0, tiled=True)

    normed = layer_norm(tokens).astype(half_type)
    joined_kv = jnp.dot(normed, kv_full, preferred_element_type=jnp.float32)
    q_prompt, q_offset, q_where = prompt_coords(dp_index * rows, rows, lengths)
    shaped = joined_kv.reshape(rows, 2, heads_dev, HEAD)
    keys = rotate(shaped[:, 0], q_offset).astype(half_type)
    values = shaped[:, 1].astype(half_type)
    own_pair = jnp.transpose(jnp.stack((keys, values)), (0, 2, 1, 3))
    plane = r_size
    back_one = shifted(own_pair, dp, plane)
    back_two = shifted(own_pair, dp, 2 * plane)
    own_first = dp_index * rows

    r_index = lax.axis_index("r")
    later = r_index < jnp.arange(plane)
    first_slot = (jnp.arange(2) == 0)[None, :]
    pick_own = (later[:, None] & first_slot)[:, :, None, None, None, None]
    pick_two = (jnp.logical_not(later)[:, None] & first_slot)[:, :, None, None, None, None]
    payload = jnp.where(
        pick_own, own_pair[None, None], jnp.where(pick_two, back_two[None, None], back_one[None, None])
    )
    payload, server_out = lax.optimization_barrier((payload, server_out))
    received = lax.all_to_all(payload, "r", 0, 0, tiled=True)
    received, rest_full = lax.optimization_barrier((received, rest_full))
    q_full = rest_full[:, :narrow]
    server_gate = rest_full[:, narrow : narrow + units]
    server_up = rest_full[:, narrow + units : narrow + 2 * units]
    server_down = down_full
    joined_q = jnp.dot(normed, q_full, preferred_element_type=jnp.float32)
    query = rotate(joined_q.reshape(rows, heads_dev, HEAD), q_offset).astype(half_type)
    query = jnp.transpose(query, (1, 0, 2))
    firsts = own_first - rows * jnp.arange(reach + 1)
    k_prompt, k_offset, k_where = jax.vmap(lambda first: prompt_coords(first, rows, lengths))(firsts)
    context = attend(r_index, query, own_pair, received, q_prompt, q_where, k_prompt, k_where)
    context = jnp.transpose(context, (1, 0, 2)).reshape(rows, narrow)

    partial_out = jnp.dot(context, server_out, preferred_element_type=jnp.float32)
    attended = scatter_sum(partial_out.astype(half_type), mp)
    slab = rows // mp_size
    own_tokens = lax.dynamic_slice_in_dim(tokens, mp_index * slab, slab, 0)
    mixed = (own_tokens.astype(jnp.float32) + attended).astype(half_type)
    normed_own = layer_norm(mixed).astype(half_type)
    normed_two = gather_by_exchange(normed_own, mp)

    gate = jnp.dot(normed_two, server_gate, preferred_element_type=jnp.float32)
    upper = jnp.dot(normed_two, server_up, preferred_element_type=jnp.float32)
    hidden = (jax.nn.silu(gate) * upper).astype(half_type)
    partial_down = jnp.dot(hidden, server_down, preferred_element_type=jnp.float32)
    share = scatter_sum(partial_down.astype(half_type), mp)
    return (mixed.astype(jnp.float32) + share).astype(half_type)


def solution(mesh):
    dp_size, mp_size = mesh.devices.shape
    y_size = mesh.devices.shape[0] // 8 if dp_size % 8 == 0 else 1
    fine = Mesh(mesh.devices.reshape(y_size, dp_size // y_size, mp_size), ("y", "r", "mp"))
    dp = ("y", "r")
    in_specs = (
        P(dp, None),
        P(),
        P(dp, "mp"),
        P(dp, "mp"),
        P(dp, "mp"),
        P(dp, "mp"),
        P(dp, "mp"),
        P(dp, "mp"),
        P(dp, "mp"),
    )
    out_specs = P(("y", "r", "mp"), None)
    return jax.shard_map(
        on_device, mesh=fine, in_specs=in_specs, out_specs=out_specs, check_vma=False
    )
```
